32 devices in a mesh: gy: 4 (over z), gz: 8 (over y, x, core).
Axes of the slice: x: 2, y: 2, z: 4, core: 2. Of those that a mesh axis runs over, the one named last changes fastest.
Arguments:
- electric_x: float32 [64, 64, 256], P('gy', 'gz'), may hold values from -1.5 to 1.5
- electric_y: float32 [64, 64, 256], P('gy', 'gz'), may hold values from -1.5 to 1.5
- electric_z: float32 [64, 64, 256], P('gy', 'gz'), may hold values from -1.5 to 1.5
- magnetic_x: float32 [64, 64, 256], P('gy', 'gz'), may hold values from -0.024 to 0.024
- magnetic_y: float32 [64, 64, 256], P('gy', 'gz'), may hold values from -0.024 to 0.024
- magnetic_z: float32 [64, 64, 256], P('gy', 'gz'), may hold values from -0.024 to 0.024
- permittivity: float32 [64, 64, 256], P('gy', 'gz'), may hold values from 1 to 12
- conductivity: float32 [64, 64, 256], P('gy', 'gz'), may hold values from 0.05 to 2
Outputs:
- half_electric_x: float32 [64, 64, 256], P('gy', 'gz')
- half_electric_y: float32 [64, 64, 256], P('gy', 'gz')
- half_electric_z: float32 [64, 64, 256], P('gy', 'gz')
- half_magnetic_x: float32 [64, 64, 256], P('gy', 'gz')
- half_magnetic_y: float32 [64, 64, 256], P('gy', 'gz')
- half_magnetic_z: float32 [64, 64, 256], P('gy', 'gz')
The draws below stay inside these ranges and needn't reach their ends.
All inputs are finite; a program needn't handle non-finite values.
Results may differ from the reference program's by a relative error of at most 0.0003.
Values sent between devices are 32-bit elements; how exact they have to be, the bound alone decides.
No kernel may reach another device: no remote copies, remote signals or barrier semaphores. Data moves between devices by JAX's collectives and lax.ppermute only.
A program may use at most 64 MiB of HBM per device.

```python
import math
import jax
import jax.numpy as jnp
from jax import lax

NX = 256
NY = 64
NZ = 64


def block_scale(stream_key, dims, split, smallest, top_value):
    factor_of = 1.0
    for position, blocks in split:
        draws = jax.random.uniform(jax.random.fold_in(jax.random.fold_in(stream_key, 6), position), (blocks,), jnp.float32, smallest / len(split), top_value / len(split))
        factor_of = factor_of * jnp.repeat(jnp.exp(draws), dims[position] // blocks).reshape((-1,) + (1,) * (len(dims) - 1 - position))
    return factor_of


def noise(key, extent, spread, reach, split=(), dtype=jnp.bfloat16):
    values = jax.random.normal(key, extent, jnp.float32) * spread
    if len(split) > 0:
        values = block_scale(key, extent, split, -0.22, 0.18) * values
    return jnp.clip(values, min=-reach, max=reach).astype(dtype)


def setup_inputs(seed: int = 0) -> dict:
    splits = jax.random.split(jax.random.key(seed), 9)
    electric_x = noise(splits[0], (NY, NZ, NX), 0.25, 1.5, ((0, 4), (1, 8)), jnp.float32)
    electric_y = noise(splits[1], (NY, NZ, NX), 0.25, 1.5, ((0, 4), (1, 8)), jnp.float32)
    electric_z = noise(splits[2], (NY, NZ, NX), 0.25, 1.5, ((0, 4), (1, 8)), jnp.float32)
    magnetic_x = noise(splits[3], (NY, NZ, NX), 0.004, 0.024, ((0, 4), (1, 8)), jnp.float32)
    magnetic_y = noise(splits[4], (NY, NZ, NX), 0.004, 0.024, ((0, 4), (1, 8)), jnp.float32)
    magnetic_z = noise(splits[5], (NY, NZ, NX), 0.004, 0.024, ((0, 4), (1, 8)), jnp.float32)
    permittivity = jnp.clip(jnp.exp(math.log(12.0) - 2.4849066 * jax.random.uniform(splits[6], (NY, NZ, NX), jnp.float32) ** block_scale(splits[6], (NY, NZ, NX), ((0, 4), (1, 8)), -0.2, 0.2)), 1.0, 12.0)
    conductivity = jnp.clip(jnp.exp(math.log(2.0) - 3.6888794 * jax.random.uniform(splits[7], (NY, NZ, NX), jnp.float32) ** block_scale(splits[7], (NY, NZ, NX), ((0, 4), (1, 8)), -0.2, 0.2)), 0.05, 2.0)
    return {"electric_x": electric_x, "electric_y": electric_y, "electric_z": electric_z, "magnetic_x": magnetic_x, "magnetic_y": magnetic_y, "magnetic_z": magnetic_z, "permittivity": permittivity, "conductivity": conductivity}


step_ratio = 1024.0

def forward_diff(values, direction):
    length = values.shape[direction]
    ahead = jnp.concatenate([lax.slice_in_dim(values, 1, length, axis=direction), jnp.zeros_like(lax.slice_in_dim(values, 0, 1, axis=direction))], axis=direction)
    return ahead - values

def backward_diff(values, direction):
    length = values.shape[direction]
    behind = jnp.concatenate([jnp.zeros_like(lax.slice_in_dim(values, 0, 1, axis=direction)), lax.slice_in_dim(values, 0, length - 1, axis=direction)], axis=direction)
    return values - behind

def line_solve(coupling, damping, right_side, direction):
    moved_coupling = jnp.moveaxis(coupling, direction, -1)
    moved_damping = jnp.moveaxis(damping, direction, -1)
    moved_right = jnp.moveaxis(right_side, direction, -1)
    length = moved_coupling.shape[-1]
    row_index = lax.broadcasted_iota(jnp.int32, moved_coupling.shape, moved_coupling.ndim - 1)
    lower_band = jnp.where(row_index >= 1, -moved_coupling, 0.0)
    upper_band = jnp.where(row_index <= length - 2, -moved_coupling, 0.0)
    main_band = 1.0 + moved_damping + moved_coupling * jnp.where(row_index >= 1, 2.0, 1.0)
    solved = lax.linalg.tridiagonal_solve(lower_band, main_band, upper_band, moved_right[..., None])[..., 0]
    return jnp.moveaxis(solved, -1, direction)

def reference(electric_x, electric_y, electric_z, magnetic_x, magnetic_y, magnetic_z, permittivity, conductivity):
    coupling = step_ratio / permittivity
    damping = conductivity / permittivity
    keeping = 1.0 - damping
    cross_y = forward_diff(electric_y, 2)
    cross_z = forward_diff(electric_z, 0)
    cross_x = forward_diff(electric_x, 1)
    source_x = keeping * electric_x + coupling * (backward_diff(magnetic_z, 0) - backward_diff(cross_y, 0) - backward_diff(magnetic_y, 1))
    source_y = keeping * electric_y + coupling * (backward_diff(magnetic_x, 1) - backward_diff(cross_z, 1) - backward_diff(magnetic_z, 2))
    source_z = keeping * electric_z + coupling * (backward_diff(magnetic_y, 2) - backward_diff(cross_x, 2) - backward_diff(magnetic_x, 0))
    half_electric_x = line_solve(coupling, damping, source_x, 0)
    half_electric_y = line_solve(coupling, damping, source_y, 1)
    half_electric_z = line_solve(coupling, damping, source_z, 2)
    half_magnetic_x = magnetic_x + forward_diff(half_electric_y, 1) - cross_z
    half_magnetic_y = magnetic_y + forward_diff(half_electric_z, 2) - cross_x
    half_magnetic_z = magnetic_z + forward_diff(half_electric_x, 0) - cross_y
    return (half_electric_x, half_electric_y, half_electric_z, half_magnetic_x, half_magnetic_y, half_magnetic_z)
```

```python
import jax
import jax.numpy as jnp
from jax import lax
from jax.sharding import PartitionSpec as P

step_ratio = 1024.0


def passed_along(value, axis, steps):
    count = lax.axis_size(axis)
    first, last = (max(0, -steps), min(count, count - steps))
    return lax.ppermute(value, axis, [(source, source + steps) for source in range(first, last)])


def take_rows(values, direction, start, length):
    return lax.slice_in_dim(values, start, start + length, axis=direction)


def edge_zeros(values, direction):
    return jnp.zeros_like(take_rows(values, direction, 0, 1))


def ahead_diff(values, direction, beyond):
    length = values.shape[direction]
    ahead = jnp.concatenate([take_rows(values, direction, 1, length - 1), beyond], axis=direction)
    return ahead - values


def behind_diff(values, direction, before):
    length = values.shape[direction]
    behind = jnp.concatenate([before, take_rows(values, direction, 0, length - 1)], axis=direction)
    return values - behind


def rows_from_below(values, direction, stride, fill_value):
    length = values.shape[direction]
    padding = jnp.full_like(take_rows(values, direction, 0, stride), fill_value)
    return jnp.concatenate(
        [padding, take_rows(values, direction, 0, length - stride)], axis=direction
    )


def rows_from_above(values, direction, stride, fill_value):
    length = values.shape[direction]
    padding = jnp.full_like(take_rows(values, direction, 0, stride), fill_value)
    return jnp.concatenate(
        [take_rows(values, direction, stride, length - stride), padding], axis=direction
    )


def reduce_lines(lower_band, main_band, upper_band, right_side, direction):
    length = main_band.shape[direction]
    stride = 1
    while stride < length:
        low_lower = rows_from_below(lower_band, direction, stride, 0.0)
        low_main = rows_from_below(main_band, direction, stride, 1.0)
        low_upper = rows_from_below(upper_band, direction, stride, 0.0)
        low_right = rows_from_below(right_side, direction + 1, stride, 0.0)
        high_lower = rows_from_above(lower_band, direction, stride, 0.0)
        high_main = rows_from_above(main_band, direction, stride, 1.0)
        high_upper = rows_from_above(upper_band, direction, stride, 0.0)
        high_right = rows_from_above(right_side, direction + 1, stride, 0.0)
        ratio_low = -lower_band / low_main
        ratio_high = -upper_band / high_main
        right_side = right_side + ratio_low[None] * low_right + ratio_high[None] * high_right
        main_band = main_band + ratio_low * low_upper + ratio_high * high_lower
        lower_band = ratio_low * low_lower
        upper_band = ratio_high * high_upper
        stride = stride * 2
    return right_side / main_band[None]


def bands(coupling, damping, row_index, line_length):
    lower_band = jnp.where(row_index >= 1, -coupling, 0.0)
    upper_band = jnp.where(row_index <= line_length - 2, -coupling, 0.0)
    main_band = 1.0 + damping + coupling * jnp.where(row_index >= 1, 2.0, 1.0)
    return (lower_band, main_band, upper_band)


def gathered(values, axis):
    return lax.all_gather(values, axis)


def block_spikes(lower_band, main_band, upper_band, right_side, direction):
    length = main_band.shape[direction]
    row_index = lax.broadcasted_iota(jnp.int32, main_band.shape, direction)
    first_row = row_index == 0
    last_row = row_index == length - 1
    left_column = jnp.where(first_row, -lower_band, 0.0)
    right_column = jnp.where(last_row, -upper_band, 0.0)
    inner_lower = jnp.where(first_row, 0.0, lower_band)
    inner_upper = jnp.where(last_row, 0.0, upper_band)
    stacked = jnp.stack([right_side, left_column, right_column])
    return reduce_lines(inner_lower, main_band, inner_upper, stacked, direction)


def interface_sweep(coefficients, position):
    blocks = coefficients.shape[0]
    alpha = jnp.zeros_like(coefficients[0, 0])
    beta = jnp.zeros_like(alpha)
    carried = []
    for block in range(blocks):
        a0, a1, a2, b0, b1, b2 = [coefficients[block, index] for index in range(6)]
        scale = 1.0 / (1.0 - a1 * beta)
        p_term = (a0 + a1 * alpha) * scale
        q_term = a2 * scale
        carried.append((alpha, beta, p_term, q_term))
        alpha = b0 + b1 * (alpha + beta * p_term)
        beta = b1 * beta * q_term + b2
    following = jnp.zeros_like(alpha)
    firsts = [None] * blocks
    earlier_lasts = [None] * blocks
    for block in reversed(range(blocks)):
        alpha_before, beta_before, p_term, q_term = carried[block]
        first_value = p_term + q_term * following
        firsts[block] = first_value
        earlier_lasts[block] = alpha_before + beta_before * first_value
        following = first_value
    nexts = jnp.stack(firsts[1:] + [jnp.zeros_like(alpha)])
    earlier = jnp.stack(earlier_lasts)
    return (
        lax.dynamic_index_in_dim(earlier, position, 0, keepdims=False),
        lax.dynamic_index_in_dim(nexts, position, 0, keepdims=False),
    )


def partitioned(lower_band, main_band, upper_band, right_side, direction, axis):
    length = main_band.shape[direction]
    solved = block_spikes(lower_band, main_band, upper_band, right_side, direction)
    edges = jnp.concatenate(
        [take_rows(solved, direction + 1, 0, 1), take_rows(solved, direction + 1, length - 1, 1)]
    )
    everyone = gathered(edges, axis)
    earlier, following = interface_sweep(everyone, lax.axis_index(axis))
    result = solved[0] + solved[1] * earlier + solved[2] * following
    return result, following


def body(
    electric_x,
    electric_y,
    electric_z,
    magnetic_x,
    magnetic_y,
    magnetic_z,
    permittivity,
    conductivity,
):
    coupling = step_ratio / permittivity
    damping = conductivity / permittivity
    keeping = 1.0 - damping
    size_y = electric_x.shape[0]
    size_z = electric_x.shape[1]
    size_x = electric_x.shape[2]
    cross_y = ahead_diff(electric_y, 2, edge_zeros(electric_y, 2))
    below_y = passed_along(
        jnp.stack(
            [
                take_rows(magnetic_z, 0, size_y - 1, 1),
                take_rows(cross_y, 0, size_y - 1, 1),
                take_rows(magnetic_x, 0, size_y - 1, 1),
            ]
        ),
        "gy",
        1,
    )
    above_ez = passed_along(take_rows(electric_z, 0, 0, 1), "gy", -1)
    cross_z = ahead_diff(electric_z, 0, above_ez)
    below_z = passed_along(
        jnp.stack(
            [
                take_rows(magnetic_y, 1, size_z - 1, 1),
                take_rows(magnetic_x, 1, size_z - 1, 1),
                take_rows(cross_z, 1, size_z - 1, 1),
            ]
        ),
        "gz",
        1,
    )
    above_ex = passed_along(take_rows(electric_x, 1, 0, 1), "gz", -1)
    cross_x = ahead_diff(electric_x, 1, above_ex)
    source_x = keeping * electric_x + coupling * (
        behind_diff(magnetic_z, 0, below_y[0])
        - behind_diff(cross_y, 0, below_y[1])
        - behind_diff(magnetic_y, 1, below_z[0])
    )
    source_y = keeping * electric_y + coupling * (
        behind_diff(magnetic_x, 1, below_z[1])
        - behind_diff(cross_z, 1, below_z[2])
        - behind_diff(magnetic_z, 2, edge_zeros(magnetic_z, 2))
    )
    source_z = keeping * electric_z + coupling * (
        behind_diff(magnetic_y, 2, edge_zeros(magnetic_y, 2))
        - behind_diff(cross_x, 2, edge_zeros(cross_x, 2))
        - behind_diff(magnetic_x, 0, below_y[2])
    )
    index_x = lax.broadcasted_iota(jnp.int32, coupling.shape, 2)
    lower_x, main_x, upper_x = bands(coupling, damping, index_x, size_x)
    half_electric_z = reduce_lines(lower_x, main_x, upper_x, source_z[None], 2)[0]
    index_z = lax.broadcasted_iota(jnp.int32, coupling.shape, 1) + lax.axis_index("gz") * size_z
    lower_z, main_z, upper_z = bands(coupling, damping, index_z, size_z * lax.axis_size("gz"))
    half_electric_y, fresh_ey = partitioned(lower_z, main_z, upper_z, source_y, 1, "gz")
    index_y = lax.broadcasted_iota(jnp.int32, coupling.shape, 0) + lax.axis_index("gy") * size_y
    lower_y, main_y, upper_y = bands(coupling, damping, index_y, size_y * lax.axis_size("gy"))
    half_electric_x, fresh_ex = partitioned(lower_y, main_y, upper_y, source_x, 0, "gy")
    half_magnetic_x = magnetic_x + ahead_diff(half_electric_y, 1, fresh_ey) - cross_z
    half_magnetic_y = (
        magnetic_y + ahead_diff(half_electric_z, 2, edge_zeros(half_electric_z, 2)) - cross_x
    )
    half_magnetic_z = magnetic_z + ahead_diff(half_electric_x, 0, fresh_ex) - cross_y
    return (
        half_electric_x,
        half_electric_y,
        half_electric_z,
        half_magnetic_x,
        half_magnetic_y,
        half_magnetic_z,
    )


def solution(mesh):
    placed = (P("gy", "gz", None),) * 8
    return jax.shard_map(
        body,
        mesh=mesh,
        in_specs=placed,
        out_specs=(P("gy", "gz", None),) * 6,
        check_vma=False,
    )
```

```python
import jax
import jax.numpy as jnp
from jax import lax
from jax.sharding import PartitionSpec as P

step_ratio = 1024.0


def passed_along(value, axis, steps):
    count = lax.axis_size(axis)
    first, last = (max(0, -steps), min(count, count - steps))
    return lax.ppermute(value, axis, [(source, source + steps) for source in range(first, last)])


def take_rows(values, direction, start, length):
    return lax.slice_in_dim(values, start, start + length, axis=direction)


def edge_zeros(values, direction):
    return jnp.zeros_like(take_rows(values, direction, 0, 1))


def ahead_diff(values, direction, beyond):
    length = values.shape[direction]
    ahead = jnp.concatenate([take_rows(values, direction, 1, length - 1), beyond], axis=direction)
    return ahead - values


def behind_diff(values, direction, before):
    length = values.shape[direction]
    behind = jnp.concatenate([before, take_rows(values, direction, 0, length - 1)], axis=direction)
    return values - behind


def rows_from_below(values, direction, stride, fill_value):
    length = values.shape[direction]
    padding = jnp.full_like(take_rows(values, direction, 0, stride), fill_value)
    return jnp.concatenate(
        [padding, take_rows(values, direction, 0, length - stride)], axis=direction
    )


def rows_from_above(values, direction, stride, fill_value):
    length = values.shape[direction]
    padding = jnp.full_like(take_rows(values, direction, 0, stride), fill_value)
    return jnp.concatenate(
        [take_rows(values, direction, stride, length - stride), padding], axis=direction
    )


def reduce_lines(lower_band, main_band, upper_band, right_side, direction):
    length = main_band.shape[direction]
    stride = 1
    while stride < length:
        low_lower = rows_from_below(lower_band, direction, stride, 0.0)
        low_main = rows_from_below(main_band, direction, stride, 1.0)
        low_upper = rows_from_below(upper_band, direction, stride, 0.0)
        low_right = rows_from_below(right_side, direction + 1, stride, 0.0)
        high_lower = rows_from_above(lower_band, direction, stride, 0.0)
        high_main = rows_from_above(main_band, direction, stride, 1.0)
        high_upper = rows_from_above(upper_band, direction, stride, 0.0)
        high_right = rows_from_above(right_side, direction + 1, stride, 0.0)
        ratio_low = -lower_band / low_main
        ratio_high = -upper_band / high_main
        right_side = right_side + ratio_low[None] * low_right + ratio_high[None] * high_right
        main_band = main_band + ratio_low * low_upper + ratio_high * high_lower
        lower_band = ratio_low * low_lower
        upper_band = ratio_high * high_upper
        stride = stride * 2
    return right_side / main_band[None]


def bands(coupling, damping, row_index, line_length):
    lower_band = jnp.where(row_index >= 1, -coupling, 0.0)
    upper_band = jnp.where(row_index <= line_length - 2, -coupling, 0.0)
    main_band = 1.0 + damping + coupling * jnp.where(row_index >= 1, 2.0, 1.0)
    return (lower_band, main_band, upper_band)


def gathered(values, axis):
    count = lax.axis_size(axis)
    shifted = [values] + [
        lax.ppermute(values, axis, [(source, (source + shift) % count) for source in range(count)])
        for shift in range(1, count)
    ]
    return jnp.stack(shifted)


def diagonal_corner(values):
    count_y = lax.axis_size("gy")
    count_z = lax.axis_size("gz")
    pairs = [
        ((row + 1) * count_z + column - 1, row * count_z + column)
        for row in range(count_y - 1)
        for column in range(1, count_z)
    ]
    return lax.ppermute(values, ("gy", "gz"), pairs)


def block_spikes(lower_band, main_band, upper_band, right_side, direction):
    length = main_band.shape[direction]
    row_index = lax.broadcasted_iota(jnp.int32, main_band.shape, direction)
    first_row = row_index == 0
    last_row = row_index == length - 1
    left_column = jnp.where(first_row, -lower_band, 0.0)
    right_column = jnp.where(last_row, -upper_band, 0.0)
    inner_lower = jnp.where(first_row, 0.0, lower_band)
    inner_upper = jnp.where(last_row, 0.0, upper_band)
    stacked = jnp.stack([right_side, left_column, right_column])
    return reduce_lines(inner_lower, main_band, inner_upper, stacked, direction)


def interface_sweep(coefficients, position):
    blocks = coefficients.shape[0]
    alpha = jnp.zeros_like(coefficients[0, 0])
    beta = jnp.zeros_like(alpha)
    carried = []
    for block in range(blocks):
        held = lax.dynamic_index_in_dim(coefficients, (position - block) % blocks, 0, False)
        a0, a1, a2, b0, b1, b2 = [held[index] for index in range(6)]
        scale = 1.0 / (1.0 - a1 * beta)
        p_term = (a0 + a1 * alpha) * scale
        q_term = a2 * scale
        carried.append((alpha, beta, p_term, q_term))
        alpha = b0 + b1 * (alpha + beta * p_term)
        beta = b1 * beta * q_term + b2
    following = jnp.zeros_like(alpha)
    firsts = [None] * blocks
    earlier_lasts = [None] * blocks
    for block in reversed(range(blocks)):
        alpha_before, beta_before, p_term, q_term = carried[block]
        first_value = p_term + q_term * following
        firsts[block] = first_value
        earlier_lasts[block] = alpha_before + beta_before * first_value
        following = first_value
    nexts = jnp.stack(firsts[1:] + [jnp.zeros_like(alpha)])
    earlier = jnp.stack(earlier_lasts)
    return (
        lax.dynamic_index_in_dim(earlier, position, 0, keepdims=False),
        lax.dynamic_index_in_dim(nexts, position, 0, keepdims=False),
    )


def partitioned(lower_band, main_band, upper_band, right_side, direction, axis):
    length = main_band.shape[direction]
    solved = block_spikes(lower_band, main_band, upper_band, right_side, direction)
    edges = jnp.concatenate(
        [take_rows(solved, direction + 1, 0, 1), take_rows(solved, direction + 1, length - 1, 1)]
    )
    everyone = gathered(edges, axis)
    earlier, following = interface_sweep(everyone, lax.axis_index(axis))
    result = solved[0] + solved[1] * earlier + solved[2] * following
    return result, following


def body(
    electric_x,
    electric_y,
    electric_z,
    magnetic_x,
    magnetic_y,
    magnetic_z,
    permittivity,
    conductivity,
):
    coupling = step_ratio / permittivity
    damping = conductivity / permittivity
    keeping = 1.0 - damping
    size_y = electric_x.shape[0]
    size_z = electric_x.shape[1]
    size_x = electric_x.shape[2]
    cross_y = ahead_diff(electric_y, 2, edge_zeros(electric_y, 2))
    below_y = passed_along(
        jnp.stack(
            [
                take_rows(magnetic_z, 0, size_y - 1, 1),
                take_rows(cross_y, 0, size_y - 1, 1),
                take_rows(magnetic_x, 0, size_y - 1, 1),
            ]
        ),
        "gy",
        1,
    )
    above_ez = passed_along(take_rows(electric_z, 0, 0, 1), "gy", -1)
    cross_z = ahead_diff(electric_z, 0, above_ez)
    below_z = passed_along(
        jnp.stack(
            [
                take_rows(magnetic_y, 1, size_z - 1, 1),
                take_rows(magnetic_x, 1, size_z - 1, 1),
                take_rows(electric_z, 1, size_z - 1, 1),
            ]
        ),
        "gz",
        1,
    )
    corner = diagonal_corner(take_rows(take_rows(electric_z, 0, 0, 1), 1, size_z - 1, 1))
    cross_z_below = ahead_diff(below_z[2], 0, corner)
    above_ex = passed_along(take_rows(electric_x, 1, 0, 1), "gz", -1)
    cross_x = ahead_diff(electric_x, 1, above_ex)
    source_x = keeping * electric_x + coupling * (
        behind_diff(magnetic_z, 0, below_y[0])
        - behind_diff(cross_y, 0, below_y[1])
        - behind_diff(magnetic_y, 1, below_z[0])
    )
    source_y = keeping * electric_y + coupling * (
        behind_diff(magnetic_x, 1, below_z[1])
        - behind_diff(cross_z, 1, cross_z_below)
        - behind_diff(magnetic_z, 2, edge_zeros(magnetic_z, 2))
    )
    source_z = keeping * electric_z + coupling * (
        behind_diff(magnetic_y, 2, edge_zeros(magnetic_y, 2))
        - behind_diff(cross_x, 2, edge_zeros(cross_x, 2))
        - behind_diff(magnetic_x, 0, below_y[2])
    )
    index_x = lax.broadcasted_iota(jnp.int32, coupling.shape, 2)
    lower_x, main_x, upper_x = bands(coupling, damping, index_x, size_x)
    half_electric_z = reduce_lines(lower_x, main_x, upper_x, source_z[None], 2)[0]
    index_z = lax.broadcasted_iota(jnp.int32, coupling.shape, 1) + lax.axis_index("gz") * size_z
    lower_z, main_z, upper_z = bands(coupling, damping, index_z, size_z * lax.axis_size("gz"))
    half_electric_y, fresh_ey = partitioned(lower_z, main_z, upper_z, source_y, 1, "gz")
    index_y = lax.broadcasted_iota(jnp.int32, coupling.shape, 0) + lax.axis_index("gy") * size_y
    lower_y, main_y, upper_y = bands(coupling, damping, index_y, size_y * lax.axis_size("gy"))
    half_electric_x, fresh_ex = partitioned(lower_y, main_y, upper_y, source_x, 0, "gy")
    half_magnetic_x = magnetic_x + ahead_diff(half_electric_y, 1, fresh_ey) - cross_z
    half_magnetic_y = (
        magnetic_y + ahead_diff(half_electric_z, 2, edge_zeros(half_electric_z, 2)) - cross_x
    )
    half_magnetic_z = magnetic_z + ahead_diff(half_electric_x, 0, fresh_ex) - cross_y
    return (
        half_electric_x,
        half_electric_y,
        half_electric_z,
        half_magnetic_x,
        half_magnetic_y,
        half_magnetic_z,
    )


def solution(mesh):
    placed = (P("gy", "gz", None),) * 8
    return jax.shard_map(
        body,
        mesh=mesh,
        in_specs=placed,
        out_specs=(P("gy", "gz", None),) * 6,
        check_vma=False,
    )
```

```python
import jax
import jax.numpy as jnp
from jax import lax
from jax.sharding import PartitionSpec as P

step_ratio = 1024.0


def passed_along(value, axis, steps):
    count = lax.axis_size(axis)
    first, last = (max(0, -steps), min(count, count - steps))
    return lax.ppermute(value, axis, [(source, source + steps) for source in range(first, last)])


def take_rows(values, direction, start, length):
    return lax.slice_in_dim(values, start, start + length, axis=direction)


def edge_zeros(values, direction):
    return jnp.zeros_like(take_rows(values, direction, 0, 1))


def ahead_diff(values, direction, beyond):
    length = values.shape[direction]
    ahead = jnp.concatenate([take_rows(values, direction, 1, length - 1), beyond], axis=direction)
    return ahead - values


def behind_diff(values, direction, before):
    length = values.shape[direction]
    behind = jnp.concatenate([before, take_rows(values, direction, 0, length - 1)], axis=direction)
    return values - behind


def rows_from_below(values, direction, stride, fill_value):
    length = values.shape[direction]
    padding = jnp.full_like(take_rows(values, direction, 0, stride), fill_value)
    return jnp.concatenate(
        [padding, take_rows(values, direction, 0, length - stride)], axis=direction
    )


def rows_from_above(values, direction, stride, fill_value):
    length = values.shape[direction]
    padding = jnp.full_like(take_rows(values, direction, 0, stride), fill_value)
    return jnp.concatenate(
        [take_rows(values, direction, stride, length - stride), padding], axis=direction
    )


def reduce_lines(lower_band, main_band, upper_band, right_side, direction):
    length = main_band.shape[direction]
    stride = 1
    while stride < length:
        low_lower = rows_from_below(lower_band, direction, stride, 0.0)
        low_main = rows_from_below(main_band, direction, stride, 1.0)
        low_upper = rows_from_below(upper_band, direction, stride, 0.0)
        low_right = rows_from_below(right_side, direction + 1, stride, 0.0)
        high_lower = rows_from_above(lower_band, direction, stride, 0.0)
        high_main = rows_from_above(main_band, direction, stride, 1.0)
        high_upper = rows_from_above(upper_band, direction, stride, 0.0)
        high_right = rows_from_above(right_side, direction + 1, stride, 0.0)
        ratio_low = -lower_band / low_main
        ratio_high = -upper_band / high_main
        right_side = right_side + ratio_low[None] * low_right + ratio_high[None] * high_right
        main_band = main_band + ratio_low * low_upper + ratio_high * high_lower
        lower_band = ratio_low * low_lower
        upper_band = ratio_high * high_upper
        stride = stride * 2
    return right_side / main_band[None]


def bands(coupling, damping, row_index, line_length):
    lower_band = jnp.where(row_index >= 1, -coupling, 0.0)
    upper_band = jnp.where(row_index <= line_length - 2, -coupling, 0.0)
    main_band = 1.0 + damping + coupling * jnp.where(row_index >= 1, 2.0, 1.0)
    return (lower_band, main_band, upper_band)


def gathered(values, axis):
    count = lax.axis_size(axis)
    shifted = [values] + [
        lax.ppermute(values, axis, [(source, (source + shift) % count) for source in range(count)])
        for shift in range(1, count)
    ]
    return jnp.stack(shifted)


def block_spikes(lower_band, main_band, upper_band, right_side, direction):
    length = main_band.shape[direction]
    row_index = lax.broadcasted_iota(jnp.int32, main_band.shape, direction)
    first_row = row_index == 0
    last_row = row_index == length - 1
    left_column = jnp.where(first_row, -lower_band, 0.0)
    right_column = jnp.where(last_row, -upper_band, 0.0)
    inner_lower = jnp.where(first_row, 0.0, lower_band)
    inner_upper = jnp.where(last_row, 0.0, upper_band)
    stacked = jnp.stack([right_side, left_column, right_column])
    return reduce_lines(inner_lower, main_band, inner_upper, stacked, direction)


def interface_sweep(coefficients, position):
    blocks = coefficients.shape[0]
    alpha = jnp.zeros_like(coefficients[0, 0])
    beta = jnp.zeros_like(alpha)
    handed = jnp.zeros_like(alpha)
    carried = []
    for block in range(blocks):
        held = lax.dynamic_index_in_dim(coefficients, (position - block) % blocks, 0, False)
        a0, a1, a2, b0, b1, b2, passed = [held[index] for index in range(7)]
        alpha = alpha + handed
        handed = passed
        scale = 1.0 / (1.0 - a1 * beta)
        p_term = (a0 + a1 * alpha) * scale
        q_term = a2 * scale
        carried.append((alpha, beta, p_term, q_term))
        alpha = b0 + b1 * (alpha + beta * p_term)
        beta = b1 * beta * q_term + b2
    following = jnp.zeros_like(alpha)
    firsts = [None] * blocks
    earlier_lasts = [None] * blocks
    for block in reversed(range(blocks)):
        alpha_before, beta_before, p_term, q_term = carried[block]
        first_value = p_term + q_term * following
        firsts[block] = first_value
        earlier_lasts[block] = alpha_before + beta_before * first_value
        following = first_value
    nexts = jnp.stack(firsts[1:] + [jnp.zeros_like(alpha)])
    earlier = jnp.stack(earlier_lasts)
    return (
        lax.dynamic_index_in_dim(earlier, position, 0, keepdims=False),
        lax.dynamic_index_in_dim(nexts, position, 0, keepdims=False),
    )


def partitioned(lower_band, main_band, upper_band, right_side, direction, axis, handed_on):
    length = main_band.shape[direction]
    solved = block_spikes(lower_band, main_band, upper_band, right_side, direction)
    edges = jnp.concatenate(
        [
            take_rows(solved, direction + 1, 0, 1),
            take_rows(solved, direction + 1, length - 1, 1),
            handed_on,
        ]
    )
    everyone = gathered(edges, axis)
    earlier, following = interface_sweep(everyone, lax.axis_index(axis))
    result = solved[0] + solved[1] * earlier + solved[2] * following
    return result, following


def body(
    electric_x,
    electric_y,
    electric_z,
    magnetic_x,
    magnetic_y,
    magnetic_z,
    permittivity,
    conductivity,
):
    coupling = step_ratio / permittivity
    damping = conductivity / permittivity
    keeping = 1.0 - damping
    size_y = electric_x.shape[0]
    size_z = electric_x.shape[1]
    size_x = electric_x.shape[2]
    cross_y = ahead_diff(electric_y, 2, edge_zeros(electric_y, 2))
    below_y = passed_along(
        jnp.stack(
            [
                take_rows(magnetic_z, 0, size_y - 1, 1),
                take_rows(cross_y, 0, size_y - 1, 1),
                take_rows(magnetic_x, 0, size_y - 1, 1),
            ]
        ),
        "gy",
        1,
    )
    above_ez = passed_along(take_rows(electric_z, 0, 0, 1), "gy", -1)
    cross_z = ahead_diff(electric_z, 0, above_ez)
    below_z = passed_along(
        jnp.stack(
            [
                take_rows(magnetic_y, 1, size_z - 1, 1),
                take_rows(magnetic_x, 1, size_z - 1, 1),
                take_rows(electric_z, 1, size_z - 1, 1),
            ]
        ),
        "gz",
        1,
    )
    cross_z_below = ahead_diff(below_z[2], 0, edge_zeros(below_z[2], 0))
    corner = jnp.where(
        lax.broadcasted_iota(jnp.int32, (size_y, 1, size_x), 0) == size_y - 1,
        take_rows(above_ez[:, size_z - 1 :], 0, 0, 1),
        0.0,
    )
    above_ex = passed_along(take_rows(electric_x, 1, 0, 1), "gz", -1)
    cross_x = ahead_diff(electric_x, 1, above_ex)
    source_x = keeping * electric_x + coupling * (
        behind_diff(magnetic_z, 0, below_y[0])
        - behind_diff(cross_y, 0, below_y[1])
        - behind_diff(magnetic_y, 1, below_z[0])
    )
    source_y = keeping * electric_y + coupling * (
        behind_diff(magnetic_x, 1, below_z[1])
        - behind_diff(cross_z, 1, cross_z_below)
        - behind_diff(magnetic_z, 2, edge_zeros(magnetic_z, 2))
    )
    source_z = keeping * electric_z + coupling * (
        behind_diff(magnetic_y, 2, edge_zeros(magnetic_y, 2))
        - behind_diff(cross_x, 2, edge_zeros(cross_x, 2))
        - behind_diff(magnetic_x, 0, below_y[2])
    )
    index_x = lax.broadcasted_iota(jnp.int32, coupling.shape, 2)
    lower_x, main_x, upper_x = bands(coupling, damping, index_x, size_x)
    half_electric_z = reduce_lines(lower_x, main_x, upper_x, source_z[None], 2)[0]
    index_z = lax.broadcasted_iota(jnp.int32, coupling.shape, 1) + lax.axis_index("gz") * size_z
    lower_z, main_z, upper_z = bands(coupling, damping, index_z, size_z * lax.axis_size("gz"))
    half_electric_y, fresh_ey = partitioned(
        lower_z, main_z, upper_z, source_y, 1, "gz", corner[None]
    )
    index_y = lax.broadcasted_iota(jnp.int32, coupling.shape, 0) + lax.axis_index("gy") * size_y
    lower_y, main_y, upper_y = bands(coupling, damping, index_y, size_y * lax.axis_size("gy"))
    half_electric_x, fresh_ex = partitioned(
        lower_y, main_y, upper_y, source_x, 0, "gy", jnp.zeros_like(source_x[None, :1])
    )
    half_magnetic_x = magnetic_x + ahead_diff(half_electric_y, 1, fresh_ey) - cross_z
    half_magnetic_y = (
        magnetic_y + ahead_diff(half_electric_z, 2, edge_zeros(half_electric_z, 2)) - cross_x
    )
    half_magnetic_z = magnetic_z + ahead_diff(half_electric_x, 0, fresh_ex) - cross_y
    return (
        half_electric_x,
        half_electric_y,
        half_electric_z,
        half_magnetic_x,
        half_magnetic_y,
        half_magnetic_z,
    )


def solution(mesh):
    placed = (P("gy", "gz", None),) * 8
    return jax.shard_map(
        body,
        mesh=mesh,
        in_specs=placed,
        out_specs=(P("gy", "gz", None),) * 6,
        check_vma=False,
    )
```

```python
import jax
import jax.numpy as jnp
from jax import lax
from jax.sharding import PartitionSpec as P

step_ratio = 1024.0


def passed_along(value, axis, steps):
    count = lax.axis_size(axis)
    first, last = (max(0, -steps), min(count, count - steps))
    return lax.ppermute(value, axis, [(source, source + steps) for source in range(first, last)])


def take_rows(values, direction, start, length):
    return lax.slice_in_dim(values, start, start + length, axis=direction)


def edge_zeros(values, direction):
    return jnp.zeros_like(take_rows(values, direction, 0, 1))


def ahead_diff(values, direction, beyond):
    length = values.shape[direction]
    ahead = jnp.concatenate([take_rows(values, direction, 1, length - 1), beyond], axis=direction)
    return ahead - values


def behind_diff(values, direction, before):
    length = values.shape[direction]
    behind = jnp.concatenate([before, take_rows(values, direction, 0, length - 1)], axis=direction)
    return values - behind


def rows_from_below(values, direction, stride, fill_value):
    length = values.shape[direction]
    padding = jnp.full_like(take_rows(values, direction, 0, stride), fill_value)
    return jnp.concatenate(
        [padding, take_rows(values, direction, 0, length - stride)], axis=direction
    )


def rows_from_above(values, direction, stride, fill_value):
    length = values.shape[direction]
    padding = jnp.full_like(take_rows(values, direction, 0, stride), fill_value)
    return jnp.concatenate(
        [take_rows(values, direction, stride, length - stride), padding], axis=direction
    )


def reduce_lines(lower_band, main_band, upper_band, right_side, direction):
    length = main_band.shape[direction]
    stride = 1
    while stride < length:
        low_lower = rows_from_below(lower_band, direction, stride, 0.0)
        low_main = rows_from_below(main_band, direction, stride, 1.0)
        low_upper = rows_from_below(upper_band, direction, stride, 0.0)
        low_right = rows_from_below(right_side, direction + 1, stride, 0.0)
        high_lower = rows_from_above(lower_band, direction, stride, 0.0)
        high_main = rows_from_above(main_band, direction, stride, 1.0)
        high_upper = rows_from_above(upper_band, direction, stride, 0.0)
        high_right = rows_from_above(right_side, direction + 1, stride, 0.0)
        ratio_low = -lower_band / low_main
        ratio_high = -upper_band / high_main
        right_side = right_side + ratio_low[None] * low_right + ratio_high[None] * high_right
        main_band = main_band + ratio_low * low_upper + ratio_high * high_lower
        lower_band = ratio_low * low_lower
        upper_band = ratio_high * high_upper
        stride = stride * 2
    return right_side / main_band[None]


def bands(coupling, damping, row_index, line_length):
    lower_band = jnp.where(row_index >= 1, -coupling, 0.0)
    upper_band = jnp.where(row_index <= line_length - 2, -coupling, 0.0)
    main_band = 1.0 + damping + coupling * jnp.where(row_index >= 1, 2.0, 1.0)
    return (lower_band, main_band, upper_band)


def gathered(values, axis):
    count = lax.axis_size(axis)
    shifted = [values] + [
        lax.ppermute(values, axis, [(source, (source + shift) % count) for source in range(count)])
        for shift in range(1, count)
    ]
    return jnp.stack(shifted)


def block_spikes(lower_band, main_band, upper_band, right_side, direction):
    length = main_band.shape[direction]
    row_index = lax.broadcasted_iota(jnp.int32, main_band.shape, direction)
    first_row = row_index == 0
    last_row = row_index == length - 1
    left_column = jnp.where(first_row, -lower_band, 0.0)
    right_column = jnp.where(last_row, -upper_band, 0.0)
    inner_lower = jnp.where(first_row, 0.0, lower_band)
    inner_upper = jnp.where(last_row, 0.0, upper_band)
    stacked = jnp.stack([right_side, left_column, right_column])
    return reduce_lines(inner_lower, main_band, inner_upper, stacked, direction)


def interface_sweep(coefficients, position):
    blocks = coefficients.shape[0]
    alpha = jnp.zeros_like(coefficients[0, 0])
    beta = jnp.zeros_like(alpha)
    handed = jnp.zeros_like(alpha)
    carried = []
    for block in range(blocks):
        held = lax.dynamic_index_in_dim(coefficients, (position - block) % blocks, 0, False)
        a0, a1, a2, b0, b1, b2, passed = [held[index] for index in range(7)]
        alpha = alpha + handed
        handed = passed
        scale = 1.0 / (1.0 - a1 * beta)
        p_term = (a0 + a1 * alpha) * scale
        q_term = a2 * scale
        carried.append((alpha, beta, p_term, q_term))
        alpha = b0 + b1 * (alpha + beta * p_term)
        beta = b1 * beta * q_term + b2
    following = jnp.zeros_like(alpha)
    firsts = [None] * blocks
    earlier_lasts = [None] * blocks
    for block in reversed(range(blocks)):
        alpha_before, beta_before, p_term, q_term = carried[block]
        first_value = p_term + q_term * following
        firsts[block] = first_value
        earlier_lasts[block] = alpha_before + beta_before * first_value
        following = first_value
    nexts = jnp.stack(firsts[1:] + [jnp.zeros_like(alpha)])
    earlier = jnp.stack(earlier_lasts)
    return (
        lax.dynamic_index_in_dim(earlier, position, 0, keepdims=False),
        lax.dynamic_index_in_dim(nexts, position, 0, keepdims=False),
    )


def partitioned(lower_band, main_band, upper_band, right_side, direction, axis, handed_on):
    length = main_band.shape[direction]
    solved = block_spikes(lower_band, main_band, upper_band, right_side, direction)
    edges = jnp.concatenate(
        [
            take_rows(solved, direction + 1, 0, 1),
            take_rows(solved, direction + 1, length - 1, 1),
            handed_on,
        ]
    )
    everyone = gathered(edges, axis)
    earlier, following = interface_sweep(everyone, lax.axis_index(axis))
    result = solved[0] + solved[1] * earlier + solved[2] * following
    return result, following


def body(
    electric_x,
    electric_y,
    electric_z,
    magnetic_x,
    magnetic_y,
    magnetic_z,
    permittivity,
    conductivity,
):
    coupling = step_ratio / permittivity
    damping = conductivity / permittivity
    keeping = 1.0 - damping
    size_y = electric_x.shape[0]
    size_z = electric_x.shape[1]
    size_x = electric_x.shape[2]
    cross_y = ahead_diff(electric_y, 2, edge_zeros(electric_y, 2))
    below_y = passed_along(
        jnp.stack(
            [
                take_rows(magnetic_z, 0, size_y - 1, 1),
                take_rows(cross_y, 0, size_y - 1, 1),
                take_rows(magnetic_x, 0, size_y - 1, 1),
            ]
        ),
        "gy",
        1,
    )
    above_ez = passed_along(take_rows(electric_z, 0, 0, 1), "gy", -1)
    below_z = passed_along(
        jnp.stack(
            [
                take_rows(magnetic_y, 1, size_z - 1, 1),
                take_rows(magnetic_x, 1, size_z - 1, 1),
                take_rows(electric_z, 1, size_z - 1, 1),
            ]
        ),
        "gz",
        1,
    )
    cross_z_below = ahead_diff(below_z[2], 0, edge_zeros(below_z[2], 0))
    corner = jnp.where(
        lax.broadcasted_iota(jnp.int32, (size_y, 1, size_x), 0) == size_y - 1,
        take_rows(above_ez[:, size_z - 1 :], 0, 0, 1),
        0.0,
    )
    above_ex = passed_along(take_rows(electric_x, 1, 0, 1), "gz", -1)
    below_y, above_ez, below_z, above_ex = lax.optimization_barrier(
        (below_y, above_ez, below_z, above_ex)
    )
    cross_z = ahead_diff(electric_z, 0, above_ez)
    cross_x = ahead_diff(electric_x, 1, above_ex)
    source_x = keeping * electric_x + coupling * (
        behind_diff(magnetic_z, 0, below_y[0])
        - behind_diff(cross_y, 0, below_y[1])
        - behind_diff(magnetic_y, 1, below_z[0])
    )
    source_y = keeping * electric_y + coupling * (
        behind_diff(magnetic_x, 1, below_z[1])
        - behind_diff(cross_z, 1, cross_z_below)
        - behind_diff(magnetic_z, 2, edge_zeros(magnetic_z, 2))
    )
    source_z = keeping * electric_z + coupling * (
        behind_diff(magnetic_y, 2, edge_zeros(magnetic_y, 2))
        - behind_diff(cross_x, 2, edge_zeros(cross_x, 2))
        - behind_diff(magnetic_x, 0, below_y[2])
    )
    index_x = lax.broadcasted_iota(jnp.int32, coupling.shape, 2)
    lower_x, main_x, upper_x = bands(coupling, damping, index_x, size_x)
    half_electric_z = reduce_lines(lower_x, main_x, upper_x, source_z[None], 2)[0]
    index_z = lax.broadcasted_iota(jnp.int32, coupling.shape, 1) + lax.axis_index("gz") * size_z
    lower_z, main_z, upper_z = bands(coupling, damping, index_z, size_z * lax.axis_size("gz"))
    half_electric_y, fresh_ey = partitioned(
        lower_z, main_z, upper_z, source_y, 1, "gz", corner[None]
    )
    index_y = lax.broadcasted_iota(jnp.int32, coupling.shape, 0) + lax.axis_index("gy") * size_y
    lower_y, main_y, upper_y = bands(coupling, damping, index_y, size_y * lax.axis_size("gy"))
    half_electric_x, fresh_ex = partitioned(
        lower_y, main_y, upper_y, source_x, 0, "gy", jnp.zeros_like(source_x[None, :1])
    )
    half_magnetic_x = magnetic_x + ahead_diff(half_electric_y, 1, fresh_ey) - cross_z
    half_magnetic_y = (
        magnetic_y + ahead_diff(half_electric_z, 2, edge_zeros(half_electric_z, 2)) - cross_x
    )
    half_magnetic_z = magnetic_z + ahead_diff(half_electric_x, 0, fresh_ex) - cross_y
    return (
        half_electric_x,
        half_electric_y,
        half_electric_z,
        half_magnetic_x,
        half_magnetic_y,
        half_magnetic_z,
    )


def solution(mesh):
    placed = (P("gy", "gz", None),) * 8
    return jax.shard_map(
        body,
        mesh=mesh,
        in_specs=placed,
        out_specs=(P("gy", "gz", None),) * 6,
        check_vma=False,
    )
```

```python
import jax
import jax.numpy as jnp
from jax import lax
from jax.sharding import PartitionSpec as P

step_ratio = 1024.0


def passed_along(value, axis, steps):
    count = lax.axis_size(axis)
    first, last = (max(0, -steps), min(count, count - steps))
    return lax.ppermute(value, axis, [(source, source + steps) for source in range(first, last)])


def take_rows(values, direction, start, length):
    return lax.slice_in_dim(values, start, start + length, axis=direction)


def edge_zeros(values, direction):
    return jnp.zeros_like(take_rows(values, direction, 0, 1))


def ahead_diff(values, direction, beyond):
    length = values.shape[direction]
    ahead = jnp.concatenate([take_rows(values, direction, 1, length - 1), beyond], axis=direction)
    return ahead - values


def behind_diff(values, direction, before):
    length = values.shape[direction]
    behind = jnp.concatenate([before, take_rows(values, direction, 0, length - 1)], axis=direction)
    return values - behind


def rows_from_below(values, direction, stride, fill_value):
    length = values.shape[direction]
    padding = jnp.full_like(take_rows(values, direction, 0, stride), fill_value)
    return jnp.concatenate(
        [padding, take_rows(values, direction, 0, length - stride)], axis=direction
    )


def rows_from_above(values, direction, stride, fill_value):
    length = values.shape[direction]
    padding = jnp.full_like(take_rows(values, direction, 0, stride), fill_value)
    return jnp.concatenate(
        [take_rows(values, direction, stride, length - stride), padding], axis=direction
    )


def reduce_lines(lower_band, main_band, upper_band, right_side, direction):
    length = main_band.shape[direction]
    stride = 1
    while stride < length:
        low_lower = rows_from_below(lower_band, direction, stride, 0.0)
        low_main = rows_from_below(main_band, direction, stride, 1.0)
        low_upper = rows_from_below(upper_band, direction, stride, 0.0)
        low_right = rows_from_below(right_side, direction + 1, stride, 0.0)
        high_lower = rows_from_above(lower_band, direction, stride, 0.0)
        high_main = rows_from_above(main_band, direction, stride, 1.0)
        high_upper = rows_from_above(upper_band, direction, stride, 0.0)
        high_right = rows_from_above(right_side, direction + 1, stride, 0.0)
        ratio_low = -lower_band / low_main
        ratio_high = -upper_band / high_main
        right_side = right_side + ratio_low[None] * low_right + ratio_high[None] * high_right
        main_band = main_band + ratio_low * low_upper + ratio_high * high_lower
        lower_band = ratio_low * low_lower
        upper_band = ratio_high * high_upper
        stride = stride * 2
    return right_side / main_band[None]


def bands(coupling, damping, row_index, line_length):
    lower_band = jnp.where(row_index >= 1, -coupling, 0.0)
    upper_band = jnp.where(row_index <= line_length - 2, -coupling, 0.0)
    main_band = 1.0 + damping + coupling * jnp.where(row_index >= 1, 2.0, 1.0)
    return (lower_band, main_band, upper_band)


def gathered(values, axis):
    count = lax.axis_size(axis)
    shifted = [values] + [
        lax.ppermute(values, axis, [(source, (source + shift) % count) for source in range(count)])
        for shift in range(1, count)
    ]
    return jnp.stack(shifted)


def block_spikes(lower_band, main_band, upper_band, right_side, direction):
    length = main_band.shape[direction]
    row_index = lax.broadcasted_iota(jnp.int32, main_band.shape, direction)
    first_row = row_index == 0
    last_row = row_index == length - 1
    left_column = jnp.where(first_row, -lower_band, 0.0)
    right_column = jnp.where(last_row, -upper_band, 0.0)
    inner_lower = jnp.where(first_row, 0.0, lower_band)
    inner_upper = jnp.where(last_row, 0.0, upper_band)
    stacked = jnp.stack([right_side, left_column, right_column])
    return reduce_lines(inner_lower, main_band, inner_upper, stacked, direction)


def interface_sweep(coefficients, position):
    blocks = coefficients.shape[0]
    alpha = jnp.zeros_like(coefficients[0, 0])
    beta = jnp.zeros_like(alpha)
    handed = jnp.zeros_like(alpha)
    carried = []
    for block in range(blocks):
        held = lax.dynamic_index_in_dim(coefficients, (position - block) % blocks, 0, False)
        a0, a1, a2, b0, b1, b2, passed = [held[index] for index in range(7)]
        alpha = alpha + handed
        handed = passed
        scale = 1.0 / (1.0 - a1 * beta)
        p_term = (a0 + a1 * alpha) * scale
        q_term = a2 * scale
        carried.append((alpha, beta, p_term, q_term))
        alpha = b0 + b1 * (alpha + beta * p_term)
        beta = b1 * beta * q_term + b2
    following = jnp.zeros_like(alpha)
    firsts = [None] * blocks
    earlier_lasts = [None] * blocks
    for block in reversed(range(blocks)):
        alpha_before, beta_before, p_term, q_term = carried[block]
        first_value = p_term + q_term * following
        firsts[block] = first_value
        earlier_lasts[block] = alpha_before + beta_before * first_value
        following = first_value
    nexts = jnp.stack(firsts[1:] + [jnp.zeros_like(alpha)])
    earlier = jnp.stack(earlier_lasts)
    return (
        lax.dynamic_index_in_dim(earlier, position, 0, keepdims=False),
        lax.dynamic_index_in_dim(nexts, position, 0, keepdims=False),
    )


def partitioned(lower_band, main_band, upper_band, right_side, direction, axis, handed_on):
    length = main_band.shape[direction]
    solved = block_spikes(lower_band, main_band, upper_band, right_side, direction)
    edges = jnp.concatenate(
        [
            take_rows(solved, direction + 1, 0, 1),
            take_rows(solved, direction + 1, length - 1, 1),
            handed_on,
        ]
    )
    everyone = gathered(edges, axis)
    earlier, following = interface_sweep(everyone, lax.axis_index(axis))
    result = solved[0] + solved[1] * earlier + solved[2] * following
    return result, following


def body(
    electric_x,
    electric_y,
    electric_z,
    magnetic_x,
    magnetic_y,
    magnetic_z,
    permittivity,
    conductivity,
):
    coupling = step_ratio / permittivity
    damping = conductivity / permittivity
    keeping = 1.0 - damping
    size_y = electric_x.shape[0]
    size_z = electric_x.shape[1]
    size_x = electric_x.shape[2]
    cross_y = ahead_diff(electric_y, 2, edge_zeros(electric_y, 2))
    below_y = passed_along(
        jnp.stack(
            [
                take_rows(magnetic_z, 0, size_y - 1, 1),
                take_rows(cross_y, 0, size_y - 1, 1),
                take_rows(magnetic_x, 0, size_y - 1, 1),
            ]
        ),
        "gy",
        1,
    )
    above_ez = passed_along(take_rows(electric_z, 0, 0, 1), "gy", -1)
    below_z = passed_along(
        jnp.stack(
            [
                take_rows(magnetic_y, 1, size_z - 1, 1),
                take_rows(magnetic_x, 1, size_z - 1, 1),
                take_rows(electric_z, 1, size_z - 1, 1),
            ]
        ),
        "gz",
        1,
    )
    cross_z_below = ahead_diff(below_z[2], 0, edge_zeros(below_z[2], 0))
    corner = jnp.where(
        lax.broadcasted_iota(jnp.int32, (size_y, 1, size_x), 0) == size_y - 1,
        take_rows(above_ez[:, size_z - 1 :], 0, 0, 1),
        0.0,
    )
    above_ex = passed_along(take_rows(electric_x, 1, 0, 1), "gz", -1)
    below_y, above_ez, below_z, above_ex = lax.optimization_barrier(
        (below_y, above_ez, below_z, above_ex)
    )
    cross_z = ahead_diff(electric_z, 0, above_ez)
    cross_x = ahead_diff(electric_x, 1, above_ex)
    source_x = keeping * electric_x + coupling * (
        behind_diff(magnetic_z, 0, below_y[0])
        - behind_diff(cross_y, 0, below_y[1])
        - behind_diff(magnetic_y, 1, below_z[0])
    )
    source_y = keeping * electric_y + coupling * (
        behind_diff(magnetic_x, 1, below_z[1])
        - behind_diff(cross_z, 1, cross_z_below)
        - behind_diff(magnetic_z, 2, edge_zeros(magnetic_z, 2))
    )
    source_z = keeping * electric_z + coupling * (
        behind_diff(magnetic_y, 2, edge_zeros(magnetic_y, 2))
        - behind_diff(cross_x, 2, edge_zeros(cross_x, 2))
        - behind_diff(magnetic_x, 0, below_y[2])
    )
    index_z = lax.broadcasted_iota(jnp.int32, coupling.shape, 1) + lax.axis_index("gz") * size_z
    lower_z, main_z, upper_z = bands(coupling, damping, index_z, size_z * lax.axis_size("gz"))
    half_electric_y, fresh_ey = partitioned(
        lower_z, main_z, upper_z, source_y, 1, "gz", corner[None]
    )
    index_y = lax.broadcasted_iota(jnp.int32, coupling.shape, 0) + lax.axis_index("gy") * size_y
    lower_y, main_y, upper_y = bands(coupling, damping, index_y, size_y * lax.axis_size("gy"))
    half_electric_x, fresh_ex = partitioned(
        lower_y, main_y, upper_y, source_x, 0, "gy", jnp.zeros_like(source_x[None, :1])
    )
    source_z, _ = lax.optimization_barrier((source_z, fresh_ex))
    index_x = lax.broadcasted_iota(jnp.int32, coupling.shape, 2)
    lower_x, main_x, upper_x = bands(coupling, damping, index_x, size_x)
    half_electric_z = reduce_lines(lower_x, main_x, upper_x, source_z[None], 2)[0]
    half_magnetic_x = magnetic_x + ahead_diff(half_electric_y, 1, fresh_ey) - cross_z
    half_magnetic_y = (
        magnetic_y + ahead_diff(half_electric_z, 2, edge_zeros(half_electric_z, 2)) - cross_x
    )
    half_magnetic_z = magnetic_z + ahead_diff(half_electric_x, 0, fresh_ex) - cross_y
    return (
        half_electric_x,
        half_electric_y,
        half_electric_z,
        half_magnetic_x,
        half_magnetic_y,
        half_magnetic_z,
    )


def solution(mesh):
    placed = (P("gy", "gz", None),) * 8
    return jax.shard_map(
        body,
        mesh=mesh,
        in_specs=placed,
        out_specs=(P("gy", "gz", None),) * 6,
        check_vma=False,
    )
```

```python
import jax
import jax.numpy as jnp
from jax import lax
from jax.sharding import PartitionSpec as P

step_ratio = 1024.0
LIMIT = 2


def passed_along(value, axis, steps):
    count = lax.axis_size(axis)
    first, last = (max(0, -steps), min(count, count - steps))
    return lax.ppermute(value, axis, [(source, source + steps) for source in range(first, last)])


def take_rows(values, direction, start, length):
    return lax.slice_in_dim(values, start, start + length, axis=direction)


def edge_zeros(values, direction):
    return jnp.zeros_like(take_rows(values, direction, 0, 1))


def ahead_diff(values, direction, beyond):
    length = values.shape[direction]
    ahead = jnp.concatenate([take_rows(values, direction, 1, length - 1), beyond], axis=direction)
    return ahead - values


def behind_diff(values, direction, before):
    length = values.shape[direction]
    behind = jnp.concatenate([before, take_rows(values, direction, 0, length - 1)], axis=direction)
    return values - behind


def rows_from_below(values, direction, stride, fill_value):
    length = values.shape[direction]
    padding = jnp.full_like(take_rows(values, direction, 0, stride), fill_value)
    return jnp.concatenate(
        [padding, take_rows(values, direction, 0, length - stride)], axis=direction
    )


def rows_from_above(values, direction, stride, fill_value):
    length = values.shape[direction]
    padding = jnp.full_like(take_rows(values, direction, 0, stride), fill_value)
    return jnp.concatenate(
        [take_rows(values, direction, stride, length - stride), padding], axis=direction
    )


def reduce_lines(lower_band, main_band, upper_band, right_side, direction):
    length = main_band.shape[direction]
    stride = 1
    while stride < length:
        low_lower = rows_from_below(lower_band, direction, stride, 0.0)
        low_main = rows_from_below(main_band, direction, stride, 1.0)
        low_upper = rows_from_below(upper_band, direction, stride, 0.0)
        low_right = rows_from_below(right_side, direction + 1, stride, 0.0)
        high_lower = rows_from_above(lower_band, direction, stride, 0.0)
        high_main = rows_from_above(main_band, direction, stride, 1.0)
        high_upper = rows_from_above(upper_band, direction, stride, 0.0)
        high_right = rows_from_above(right_side, direction + 1, stride, 0.0)
        ratio_low = -lower_band / low_main
        ratio_high = -upper_band / high_main
        right_side = right_side + ratio_low[None] * low_right + ratio_high[None] * high_right
        main_band = main_band + ratio_low * low_upper + ratio_high * high_lower
        lower_band = ratio_low * low_lower
        upper_band = ratio_high * high_upper
        stride = stride * 2
    return right_side / main_band[None]


def bands(coupling, damping, row_index, line_length):
    lower_band = jnp.where(row_index >= 1, -coupling, 0.0)
    upper_band = jnp.where(row_index <= line_length - 2, -coupling, 0.0)
    main_band = 1.0 + damping + coupling * jnp.where(row_index >= 1, 2.0, 1.0)
    return (lower_band, main_band, upper_band)


def gathered(values, axis):
    count = lax.axis_size(axis)
    direct = count if count <= LIMIT else (count + 1) // 2
    shifted = jnp.stack(
        [values]
        + [
            lax.ppermute(values, axis, [(source, (source + shift) % count) for source in range(count)])
            for shift in range(1, direct)
        ]
    )
    while shifted.shape[0] < count:
        have = shifted.shape[0]
        moved = lax.ppermute(shifted, axis, [(source, (source + have) % count) for source in range(count)])
        shifted = jnp.concatenate([shifted, moved])[:count]
    return shifted


def block_spikes(lower_band, main_band, upper_band, right_side, direction):
    length = main_band.shape[direction]
    row_index = lax.broadcasted_iota(jnp.int32, main_band.shape, direction)
    first_row = row_index == 0
    last_row = row_index == length - 1
    left_column = jnp.where(first_row, -lower_band, 0.0)
    right_column = jnp.where(last_row, -upper_band, 0.0)
    inner_lower = jnp.where(first_row, 0.0, lower_band)
    inner_upper = jnp.where(last_row, 0.0, upper_band)
    stacked = jnp.stack([right_side, left_column, right_column])
    return reduce_lines(inner_lower, main_band, inner_upper, stacked, direction)


def interface_sweep(coefficients, position):
    blocks = coefficients.shape[0]
    alpha = jnp.zeros_like(coefficients[0, 0])
    beta = jnp.zeros_like(alpha)
    handed = jnp.zeros_like(alpha)
    carried = []
    for block in range(blocks):
        held = lax.dynamic_index_in_dim(coefficients, (position - block) % blocks, 0, False)
        a0, a1, a2, b0, b1, b2, passed = [held[index] for index in range(7)]
        alpha = alpha + handed
        handed = passed
        scale = 1.0 / (1.0 - a1 * beta)
        p_term = (a0 + a1 * alpha) * scale
        q_term = a2 * scale
        carried.append((alpha, beta, p_term, q_term))
        alpha = b0 + b1 * (alpha + beta * p_term)
        beta = b1 * beta * q_term + b2
    following = jnp.zeros_like(alpha)
    firsts = [None] * blocks
    earlier_lasts = [None] * blocks
    for block in reversed(range(blocks)):
        alpha_before, beta_before, p_term, q_term = carried[block]
        first_value = p_term + q_term * following
        firsts[block] = first_value
        earlier_lasts[block] = alpha_before + beta_before * first_value
        following = first_value
    nexts = jnp.stack(firsts[1:] + [jnp.zeros_like(alpha)])
    earlier = jnp.stack(earlier_lasts)
    return (
        lax.dynamic_index_in_dim(earlier, position, 0, keepdims=False),
        lax.dynamic_index_in_dim(nexts, position, 0, keepdims=False),
    )


def partitioned(lower_band, main_band, upper_band, right_side, direction, axis, handed_on):
    length = main_band.shape[direction]
    solved = block_spikes(lower_band, main_band, upper_band, right_side, direction)
    edges = jnp.concatenate(
        [
            take_rows(solved, direction + 1, 0, 1),
            take_rows(solved, direction + 1, length - 1, 1),
            handed_on,
        ]
    )
    everyone = gathered(edges, axis)
    earlier, following = interface_sweep(everyone, lax.axis_index(axis))
    result = solved[0] + solved[1] * earlier + solved[2] * following
    return result, following


def body(
    electric_x,
    electric_y,
    electric_z,
    magnetic_x,
    magnetic_y,
    magnetic_z,
    permittivity,
    conductivity,
):
    coupling = step_ratio / permittivity
    damping = conductivity / permittivity
    keeping = 1.0 - damping
    size_y = electric_x.shape[0]
    size_z = electric_x.shape[1]
    size_x = electric_x.shape[2]
    cross_y = ahead_diff(electric_y, 2, edge_zeros(electric_y, 2))
    below_y = passed_along(
        jnp.stack(
            [
                take_rows(magnetic_z, 0, size_y - 1, 1),
                take_rows(cross_y, 0, size_y - 1, 1),
                take_rows(magnetic_x, 0, size_y - 1, 1),
            ]
        ),
        "gy",
        1,
    )
    above_ez = passed_along(take_rows(electric_z, 0, 0, 1), "gy", -1)
    below_z = passed_along(
        jnp.stack(
            [
                take_rows(magnetic_y, 1, size_z - 1, 1),
                take_rows(magnetic_x, 1, size_z - 1, 1),
                take_rows(electric_z, 1, size_z - 1, 1),
            ]
        ),
        "gz",
        1,
    )
    cross_z_below = ahead_diff(below_z[2], 0, edge_zeros(below_z[2], 0))
    corner = jnp.where(
        lax.broadcasted_iota(jnp.int32, (size_y, 1, size_x), 0) == size_y - 1,
        take_rows(above_ez[:, size_z - 1 :], 0, 0, 1),
        0.0,
    )
    above_ex = passed_along(take_rows(electric_x, 1, 0, 1), "gz", -1)
    below_y, above_ez, below_z, above_ex = lax.optimization_barrier(
        (below_y, above_ez, below_z, above_ex)
    )
    cross_z = ahead_diff(electric_z, 0, above_ez)
    cross_x = ahead_diff(electric_x, 1, above_ex)
    source_x = keeping * electric_x + coupling * (
        behind_diff(magnetic_z, 0, below_y[0])
        - behind_diff(cross_y, 0, below_y[1])
        - behind_diff(magnetic_y, 1, below_z[0])
    )
    source_y = keeping * electric_y + coupling * (
        behind_diff(magnetic_x, 1, below_z[1])
        - behind_diff(cross_z, 1, cross_z_below)
        - behind_diff(magnetic_z, 2, edge_zeros(magnetic_z, 2))
    )
    source_z = keeping * electric_z + coupling * (
        behind_diff(magnetic_y, 2, edge_zeros(magnetic_y, 2))
        - behind_diff(cross_x, 2, edge_zeros(cross_x, 2))
        - behind_diff(magnetic_x, 0, below_y[2])
    )
    index_z = lax.broadcasted_iota(jnp.int32, coupling.shape, 1) + lax.axis_index("gz") * size_z
    lower_z, main_z, upper_z = bands(coupling, damping, index_z, size_z * lax.axis_size("gz"))
    half_electric_y, fresh_ey = partitioned(
        lower_z, main_z, upper_z, source_y, 1, "gz", corner[None]
    )
    index_y = lax.broadcasted_iota(jnp.int32, coupling.shape, 0) + lax.axis_index("gy") * size_y
    lower_y, main_y, upper_y = bands(coupling, damping, index_y, size_y * lax.axis_size("gy"))
    half_electric_x, fresh_ex = partitioned(
        lower_y, main_y, upper_y, source_x, 0, "gy", jnp.zeros_like(source_x[None, :1])
    )
    source_z, _ = lax.optimization_barrier((source_z, fresh_ex))
    index_x = lax.broadcasted_iota(jnp.int32, coupling.shape, 2)
    lower_x, main_x, upper_x = bands(coupling, damping, index_x, size_x)
    half_electric_z = reduce_lines(lower_x, main_x, upper_x, source_z[None], 2)[0]
    half_magnetic_x = magnetic_x + ahead_diff(half_electric_y, 1, fresh_ey) - cross_z
    half_magnetic_y = (
        magnetic_y + ahead_diff(half_electric_z, 2, edge_zeros(half_electric_z, 2)) - cross_x
    )
    half_magnetic_z = magnetic_z + ahead_diff(half_electric_x, 0, fresh_ex) - cross_y
    return (
        half_electric_x,
        half_electric_y,
        half_electric_z,
        half_magnetic_x,
        half_magnetic_y,
        half_magnetic_z,
    )


def solution(mesh):
    placed = (P("gy", "gz", None),) * 8
    return jax.shard_map(
        body,
        mesh=mesh,
        in_specs=placed,
        out_specs=(P("gy", "gz", None),) * 6,
        check_vma=False,
    )
```

```python
import jax
import jax.numpy as jnp
from jax import lax
from jax.sharding import PartitionSpec as P

step_ratio = 1024.0
DIRECT = {8: 5}
LIMIT = 2


def passed_along(value, axis, steps):
    count = lax.axis_size(axis)
    first, last = (max(0, -steps), min(count, count - steps))
    return lax.ppermute(value, axis, [(source, source + steps) for source in range(first, last)])


def take_rows(values, direction, start, length):
    return lax.slice_in_dim(values, start, start + length, axis=direction)


def edge_zeros(values, direction):
    return jnp.zeros_like(take_rows(values, direction, 0, 1))


def ahead_diff(values, direction, beyond):
    length = values.shape[direction]
    ahead = jnp.concatenate([take_rows(values, direction, 1, length - 1), beyond], axis=direction)
    return ahead - values


def behind_diff(values, direction, before):
    length = values.shape[direction]
    behind = jnp.concatenate([before, take_rows(values, direction, 0, length - 1)], axis=direction)
    return values - behind


def rows_from_below(values, direction, stride, fill_value):
    length = values.shape[direction]
    padding = jnp.full_like(take_rows(values, direction, 0, stride), fill_value)
    return jnp.concatenate(
        [padding, take_rows(values, direction, 0, length - stride)], axis=direction
    )


def rows_from_above(values, direction, stride, fill_value):
    length = values.shape[direction]
    padding = jnp.full_like(take_rows(values, direction, 0, stride), fill_value)
    return jnp.concatenate(
        [take_rows(values, direction, stride, length - stride), padding], axis=direction
    )


def reduce_lines(lower_band, main_band, upper_band, right_side, direction):
    length = main_band.shape[direction]
    stride = 1
    while stride < length:
        low_lower = rows_from_below(lower_band, direction, stride, 0.0)
        low_main = rows_from_below(main_band, direction, stride, 1.0)
        low_upper = rows_from_below(upper_band, direction, stride, 0.0)
        low_right = rows_from_below(right_side, direction + 1, stride, 0.0)
        high_lower = rows_from_above(lower_band, direction, stride, 0.0)
        high_main = rows_from_above(main_band, direction, stride, 1.0)
        high_upper = rows_from_above(upper_band, direction, stride, 0.0)
        high_right = rows_from_above(right_side, direction + 1, stride, 0.0)
        ratio_low = -lower_band / low_main
        ratio_high = -upper_band / high_main
        right_side = right_side + ratio_low[None] * low_right + ratio_high[None] * high_right
        main_band = main_band + ratio_low * low_upper + ratio_high * high_lower
        lower_band = ratio_low * low_lower
        upper_band = ratio_high * high_upper
        stride = stride * 2
    return right_side / main_band[None]


def bands(coupling, damping, row_index, line_length):
    lower_band = jnp.where(row_index >= 1, -coupling, 0.0)
    upper_band = jnp.where(row_index <= line_length - 2, -coupling, 0.0)
    main_band = 1.0 + damping + coupling * jnp.where(row_index >= 1, 2.0, 1.0)
    return (lower_band, main_band, upper_band)


def gathered(values, axis):
    count = lax.axis_size(axis)
    direct = count if count <= LIMIT else DIRECT.get(count, (count + 1) // 2)
    shifted = jnp.stack(
        [values]
        + [
            lax.ppermute(values, axis, [(source, (source + shift) % count) for source in range(count)])
            for shift in range(1, direct)
        ]
    )
    while shifted.shape[0] < count:
        have = shifted.shape[0]
        moved = lax.ppermute(
            shifted[: count - have], axis, [(source, (source + have) % count) for source in range(count)]
        )
        shifted = jnp.concatenate([shifted, moved])
    return shifted


def block_spikes(lower_band, main_band, upper_band, right_side, direction):
    length = main_band.shape[direction]
    row_index = lax.broadcasted_iota(jnp.int32, main_band.shape, direction)
    first_row = row_index == 0
    last_row = row_index == length - 1
    left_column = jnp.where(first_row, -lower_band, 0.0)
    right_column = jnp.where(last_row, -upper_band, 0.0)
    inner_lower = jnp.where(first_row, 0.0, lower_band)
    inner_upper = jnp.where(last_row, 0.0, upper_band)
    stacked = jnp.stack([right_side, left_column, right_column])
    return reduce_lines(inner_lower, main_band, inner_upper, stacked, direction)


def interface_sweep(coefficients, position):
    blocks = coefficients.shape[0]
    alpha = jnp.zeros_like(coefficients[0, 0])
    beta = jnp.zeros_like(alpha)
    handed = jnp.zeros_like(alpha)
    carried = []
    for block in range(blocks):
        held = lax.dynamic_index_in_dim(coefficients, (position - block) % blocks, 0, False)
        a0, a1, a2, b0, b1, b2, passed = [held[index] for index in range(7)]
        alpha = alpha + handed
        handed = passed
        scale = 1.0 / (1.0 - a1 * beta)
        p_term = (a0 + a1 * alpha) * scale
        q_term = a2 * scale
        carried.append((alpha, beta, p_term, q_term))
        alpha = b0 + b1 * (alpha + beta * p_term)
        beta = b1 * beta * q_term + b2
    following = jnp.zeros_like(alpha)
    firsts = [None] * blocks
    earlier_lasts = [None] * blocks
    for block in reversed(range(blocks)):
        alpha_before, beta_before, p_term, q_term = carried[block]
        first_value = p_term + q_term * following
        firsts[block] = first_value
        earlier_lasts[block] = alpha_before + beta_before * first_value
        following = first_value
    nexts = jnp.stack(firsts[1:] + [jnp.zeros_like(alpha)])
    earlier = jnp.stack(earlier_lasts)
    return (
        lax.dynamic_index_in_dim(earlier, position, 0, keepdims=False),
        lax.dynamic_index_in_dim(nexts, position, 0, keepdims=False),
    )


def partitioned(lower_band, main_band, upper_band, right_side, direction, axis, handed_on):
    length = main_band.shape[direction]
    solved = block_spikes(lower_band, main_band, upper_band, right_side, direction)
    edges = jnp.concatenate(
        [
            take_rows(solved, direction + 1, 0, 1),
            take_rows(solved, direction + 1, length - 1, 1),
            handed_on,
        ]
    )
    everyone = gathered(edges, axis)
    earlier, following = interface_sweep(everyone, lax.axis_index(axis))
    result = solved[0] + solved[1] * earlier + solved[2] * following
    return result, following


def body(
    electric_x,
    electric_y,
    electric_z,
    magnetic_x,
    magnetic_y,
    magnetic_z,
    permittivity,
    conductivity,
):
    coupling = step_ratio / permittivity
    damping = conductivity / permittivity
    keeping = 1.0 - damping
    size_y = electric_x.shape[0]
    size_z = electric_x.shape[1]
    size_x = electric_x.shape[2]
    cross_y = ahead_diff(electric_y, 2, edge_zeros(electric_y, 2))
    below_y = passed_along(
        jnp.stack(
            [
                take_rows(magnetic_z, 0, size_y - 1, 1),
                take_rows(cross_y, 0, size_y - 1, 1),
                take_rows(magnetic_x, 0, size_y - 1, 1),
            ]
        ),
        "gy",
        1,
    )
    above_ez = passed_along(take_rows(electric_z, 0, 0, 1), "gy", -1)
    below_z = passed_along(
        jnp.stack(
            [
                take_rows(magnetic_y, 1, size_z - 1, 1),
                take_rows(magnetic_x, 1, size_z - 1, 1),
                take_rows(electric_z, 1, size_z - 1, 1),
            ]
        ),
        "gz",
        1,
    )
    cross_z_below = ahead_diff(below_z[2], 0, edge_zeros(below_z[2], 0))
    corner = jnp.where(
        lax.broadcasted_iota(jnp.int32, (size_y, 1, size_x), 0) == size_y - 1,
        take_rows(above_ez[:, size_z - 1 :], 0, 0, 1),
        0.0,
    )
    above_ex = passed_along(take_rows(electric_x, 1, 0, 1), "gz", -1)
    below_y, above_ez, below_z, above_ex = lax.optimization_barrier(
        (below_y, above_ez, below_z, above_ex)
    )
    cross_z = ahead_diff(electric_z, 0, above_ez)
    cross_x = ahead_diff(electric_x, 1, above_ex)
    source_x = keeping * electric_x + coupling * (
        behind_diff(magnetic_z, 0, below_y[0])
        - behind_diff(cross_y, 0, below_y[1])
        - behind_diff(magnetic_y, 1, below_z[0])
    )
    source_y = keeping * electric_y + coupling * (
        behind_diff(magnetic_x, 1, below_z[1])
        - behind_diff(cross_z, 1, cross_z_below)
        - behind_diff(magnetic_z, 2, edge_zeros(magnetic_z, 2))
    )
    source_z = keeping * electric_z + coupling * (
        behind_diff(magnetic_y, 2, edge_zeros(magnetic_y, 2))
        - behind_diff(cross_x, 2, edge_zeros(cross_x, 2))
        - behind_diff(magnetic_x, 0, below_y[2])
    )
    index_z = lax.broadcasted_iota(jnp.int32, coupling.shape, 1) + lax.axis_index("gz") * size_z
    lower_z, main_z, upper_z = bands(coupling, damping, index_z, size_z * lax.axis_size("gz"))
    half_electric_y, fresh_ey = partitioned(
        lower_z, main_z, upper_z, source_y, 1, "gz", corner[None]
    )
    index_y = lax.broadcasted_iota(jnp.int32, coupling.shape, 0) + lax.axis_index("gy") * size_y
    lower_y, main_y, upper_y = bands(coupling, damping, index_y, size_y * lax.axis_size("gy"))
    half_electric_x, fresh_ex = partitioned(
        lower_y, main_y, upper_y, source_x, 0, "gy", jnp.zeros_like(source_x[None, :1])
    )
    source_z, _ = lax.optimization_barrier((source_z, fresh_ex))
    index_x = lax.broadcasted_iota(jnp.int32, coupling.shape, 2)
    lower_x, main_x, upper_x = bands(coupling, damping, index_x, size_x)
    half_electric_z = reduce_lines(lower_x, main_x, upper_x, source_z[None], 2)[0]
    half_magnetic_x = magnetic_x + ahead_diff(half_electric_y, 1, fresh_ey) - cross_z
    half_magnetic_y = (
        magnetic_y + ahead_diff(half_electric_z, 2, edge_zeros(half_electric_z, 2)) - cross_x
    )
    half_magnetic_z = magnetic_z + ahead_diff(half_electric_x, 0, fresh_ex) - cross_y
    return (
        half_electric_x,
        half_electric_y,
        half_electric_z,
        half_magnetic_x,
        half_magnetic_y,
        half_magnetic_z,
    )


def solution(mesh):
    placed = (P("gy", "gz", None),) * 8
    return jax.shard_map(
        body,
        mesh=mesh,
        in_specs=placed,
        out_specs=(P("gy", "gz", None),) * 6,
        check_vma=False,
    )
```

```python
import jax
import jax.numpy as jnp
from jax import lax
from jax.sharding import PartitionSpec as P

step_ratio = 1024.0
DIRECT = {8: 5}
HOPS = {8: ((1, 2, 3, 7), 4)}
LIMIT = 2


def passed_along(value, axis, steps):
    count = lax.axis_size(axis)
    first, last = (max(0, -steps), min(count, count - steps))
    return lax.ppermute(value, axis, [(source, source + steps) for source in range(first, last)])


def take_rows(values, direction, start, length):
    return lax.slice_in_dim(values, start, start + length, axis=direction)


def edge_zeros(values, direction):
    return jnp.zeros_like(take_rows(values, direction, 0, 1))


def ahead_diff(values, direction, beyond):
    length = values.shape[direction]
    ahead = jnp.concatenate([take_rows(values, direction, 1, length - 1), beyond], axis=direction)
    return ahead - values


def behind_diff(values, direction, before):
    length = values.shape[direction]
    behind = jnp.concatenate([before, take_rows(values, direction, 0, length - 1)], axis=direction)
    return values - behind


def rows_from_below(values, direction, stride, fill_value):
    length = values.shape[direction]
    padding = jnp.full_like(take_rows(values, direction, 0, stride), fill_value)
    return jnp.concatenate(
        [padding, take_rows(values, direction, 0, length - stride)], axis=direction
    )


def rows_from_above(values, direction, stride, fill_value):
    length = values.shape[direction]
    padding = jnp.full_like(take_rows(values, direction, 0, stride), fill_value)
    return jnp.concatenate(
        [take_rows(values, direction, stride, length - stride), padding], axis=direction
    )


def reduce_lines(lower_band, main_band, upper_band, right_side, direction):
    length = main_band.shape[direction]
    stride = 1
    while stride < length:
        low_lower = rows_from_below(lower_band, direction, stride, 0.0)
        low_main = rows_from_below(main_band, direction, stride, 1.0)
        low_upper = rows_from_below(upper_band, direction, stride, 0.0)
        low_right = rows_from_below(right_side, direction + 1, stride, 0.0)
        high_lower = rows_from_above(lower_band, direction, stride, 0.0)
        high_main = rows_from_above(main_band, direction, stride, 1.0)
        high_upper = rows_from_above(upper_band, direction, stride, 0.0)
        high_right = rows_from_above(right_side, direction + 1, stride, 0.0)
        ratio_low = -lower_band / low_main
        ratio_high = -upper_band / high_main
        right_side = right_side + ratio_low[None] * low_right + ratio_high[None] * high_right
        main_band = main_band + ratio_low * low_upper + ratio_high * high_lower
        lower_band = ratio_low * low_lower
        upper_band = ratio_high * high_upper
        stride = stride * 2
    return right_side / main_band[None]


def bands(coupling, damping, row_index, line_length):
    lower_band = jnp.where(row_index >= 1, -coupling, 0.0)
    upper_band = jnp.where(row_index <= line_length - 2, -coupling, 0.0)
    main_band = 1.0 + damping + coupling * jnp.where(row_index >= 1, 2.0, 1.0)
    return (lower_band, main_band, upper_band)


def cyclic_shift(values, axis, shift):
    count = lax.axis_size(axis)
    return lax.ppermute(values, axis, [(source, (source + shift) % count) for source in range(count)])


def gathered(values, axis):
    count = lax.axis_size(axis)
    if count in HOPS:
        direct, hop = HOPS[count]
        held = {0: values}
        for shift in direct:
            held[shift] = cyclic_shift(values, axis, shift)
        carried = [shift for shift in range(count) if shift + hop < count and shift + hop not in held]
        moved = cyclic_shift(jnp.stack([held[shift] for shift in carried]), axis, hop)
        for index, shift in enumerate(carried):
            held[shift + hop] = moved[index]
        return jnp.stack([held[shift] for shift in range(count)]), held
    direct = count if count <= LIMIT else DIRECT.get(count, (count + 1) // 2)
    pieces = [values] + [cyclic_shift(values, axis, shift) for shift in range(1, direct)]
    held = dict(enumerate(pieces))
    shifted = jnp.stack(pieces)
    while shifted.shape[0] < count:
        have = shifted.shape[0]
        moved = cyclic_shift(shifted[: count - have], axis, have)
        for index in range(moved.shape[0]):
            held[have + index] = moved[index]
        shifted = jnp.concatenate([shifted, moved])
    return shifted, held


def block_spikes(lower_band, main_band, upper_band, right_side, direction):
    length = main_band.shape[direction]
    row_index = lax.broadcasted_iota(jnp.int32, main_band.shape, direction)
    first_row = row_index == 0
    last_row = row_index == length - 1
    left_column = jnp.where(first_row, -lower_band, 0.0)
    right_column = jnp.where(last_row, -upper_band, 0.0)
    inner_lower = jnp.where(first_row, 0.0, lower_band)
    inner_upper = jnp.where(last_row, 0.0, upper_band)
    stacked = jnp.stack([right_side, left_column, right_column])
    return reduce_lines(inner_lower, main_band, inner_upper, stacked, direction)


def interface_sweep(coefficients, position):
    blocks = coefficients.shape[0]
    alpha = jnp.zeros_like(coefficients[0, 0])
    beta = jnp.zeros_like(alpha)
    handed = jnp.zeros_like(alpha)
    carried = []
    for block in range(blocks):
        held = lax.dynamic_index_in_dim(coefficients, (position - block) % blocks, 0, False)
        a0, a1, a2, b0, b1, b2, passed = [held[index] for index in range(7)]
        alpha = alpha + handed
        handed = passed
        scale = 1.0 / (1.0 - a1 * beta)
        p_term = (a0 + a1 * alpha) * scale
        q_term = a2 * scale
        carried.append((alpha, beta, p_term, q_term))
        alpha = b0 + b1 * (alpha + beta * p_term)
        beta = b1 * beta * q_term + b2
    following = jnp.zeros_like(alpha)
    firsts = [None] * blocks
    earlier_lasts = [None] * blocks
    for block in reversed(range(blocks)):
        alpha_before, beta_before, p_term, q_term = carried[block]
        first_value = p_term + q_term * following
        firsts[block] = first_value
        earlier_lasts[block] = alpha_before + beta_before * first_value
        following = first_value
    nexts = jnp.stack(firsts[1:] + [jnp.zeros_like(alpha)])
    earlier = jnp.stack(earlier_lasts)
    return (
        lax.dynamic_index_in_dim(earlier, position, 0, keepdims=False),
        lax.dynamic_index_in_dim(nexts, position, 0, keepdims=False),
    )


def partitioned(lower_band, main_band, upper_band, right_side, direction, axis, handed_on, extra):
    length = main_band.shape[direction]
    solved = block_spikes(lower_band, main_band, upper_band, right_side, direction)
    edges = jnp.concatenate(
        [
            take_rows(solved, direction + 1, 0, 1),
            take_rows(solved, direction + 1, length - 1, 1),
            handed_on,
            extra,
        ]
    )
    everyone, held = gathered(edges, axis)
    count = lax.axis_size(axis)
    position = lax.axis_index(axis)
    from_below = jnp.where(position >= 1, held[1][7], 0.0)
    from_above = jnp.where(position <= count - 2, held[count - 1][7], 0.0)
    return solved, everyone, from_below, from_above


def finished(solved, everyone, axis):
    earlier, following = interface_sweep(everyone, lax.axis_index(axis))
    return solved[0] + solved[1] * earlier + solved[2] * following, following


def body(
    electric_x,
    electric_y,
    electric_z,
    magnetic_x,
    magnetic_y,
    magnetic_z,
    permittivity,
    conductivity,
):
    coupling = step_ratio / permittivity
    damping = conductivity / permittivity
    keeping = 1.0 - damping
    size_y = electric_x.shape[0]
    size_z = electric_x.shape[1]
    size_x = electric_x.shape[2]
    cross_y = ahead_diff(electric_y, 2, edge_zeros(electric_y, 2))
    below_my = passed_along(take_rows(magnetic_y, 1, size_z - 1, 1), "gz", 1)
    above_ez = passed_along(take_rows(electric_z, 0, 0, 1), "gy", -1)
    cross_z = ahead_diff(electric_z, 0, above_ez)
    source_x = keeping * electric_x + coupling * (
        behind_diff(magnetic_z, 0, edge_zeros(magnetic_z, 0))
        - behind_diff(cross_y, 0, edge_zeros(cross_y, 0))
        - behind_diff(magnetic_y, 1, below_my)
    )
    source_y = keeping * electric_y + coupling * (
        behind_diff(magnetic_x, 1, edge_zeros(magnetic_x, 1))
        - behind_diff(cross_z, 1, edge_zeros(cross_z, 1))
        - behind_diff(magnetic_z, 2, edge_zeros(magnetic_z, 2))
    )
    index_z = lax.broadcasted_iota(jnp.int32, coupling.shape, 1) + lax.axis_index("gz") * size_z
    lower_z, main_z, upper_z = bands(coupling, damping, index_z, size_z * lax.axis_size("gz"))
    solved_z, everyone_z, _, above_ex = partitioned(
        lower_z,
        main_z,
        upper_z,
        source_y,
        1,
        "gz",
        (take_rows(cross_z, 1, size_z - 1, 1) - take_rows(magnetic_x, 1, size_z - 1, 1))[None],
        take_rows(electric_x, 1, 0, 1)[None],
    )
    index_y = lax.broadcasted_iota(jnp.int32, coupling.shape, 0) + lax.axis_index("gy") * size_y
    lower_y, main_y, upper_y = bands(coupling, damping, index_y, size_y * lax.axis_size("gy"))
    solved_y, everyone_y, below_mx, _ = partitioned(
        lower_y,
        main_y,
        upper_y,
        source_x,
        0,
        "gy",
        (take_rows(cross_y, 0, size_y - 1, 1) - take_rows(magnetic_z, 0, size_y - 1, 1))[None],
        take_rows(magnetic_x, 0, size_y - 1, 1)[None],
    )
    half_electric_x, fresh_ex = finished(solved_y, everyone_y, "gy")
    cross_x = ahead_diff(electric_x, 1, above_ex)
    source_z = keeping * electric_z + coupling * (
        behind_diff(magnetic_y, 2, edge_zeros(magnetic_y, 2))
        - behind_diff(cross_x, 2, edge_zeros(cross_x, 2))
        - behind_diff(magnetic_x, 0, below_mx)
    )
    index_x = lax.broadcasted_iota(jnp.int32, coupling.shape, 2)
    lower_x, main_x, upper_x = bands(coupling, damping, index_x, size_x)
    half_electric_z = reduce_lines(lower_x, main_x, upper_x, source_z[None], 2)[0]
    half_electric_z, everyone_z = lax.optimization_barrier((half_electric_z, everyone_z))
    half_electric_y, fresh_ey = finished(solved_z, everyone_z, "gz")
    half_magnetic_x = magnetic_x + ahead_diff(half_electric_y, 1, fresh_ey) - cross_z
    half_magnetic_y = (
        magnetic_y + ahead_diff(half_electric_z, 2, edge_zeros(half_electric_z, 2)) - cross_x
    )
    half_magnetic_z = magnetic_z + ahead_diff(half_electric_x, 0, fresh_ex) - cross_y
    return (
        half_electric_x,
        half_electric_y,
        half_electric_z,
        half_magnetic_x,
        half_magnetic_y,
        half_magnetic_z,
    )


def solution(mesh):
    placed = (P("gy", "gz", None),) * 8
    return jax.shard_map(
        body,
        mesh=mesh,
        in_specs=placed,
        out_specs=(P("gy", "gz", None),) * 6,
        check_vma=False,
    )
```

```python
import jax
import jax.numpy as jnp
from jax import lax
from jax.sharding import PartitionSpec as P

step_ratio = 1024.0
DIRECT = {8: 5}
HOPS = {8: ((1, 2, 3, 4, 7), 5)}
LIMIT = 2


def passed_along(value, axis, steps):
    count = lax.axis_size(axis)
    first, last = (max(0, -steps), min(count, count - steps))
    return lax.ppermute(value, axis, [(source, source + steps) for source in range(first, last)])


def take_rows(values, direction, start, length):
    return lax.slice_in_dim(values, start, start + length, axis=direction)


def edge_zeros(values, direction):
    return jnp.zeros_like(take_rows(values, direction, 0, 1))


def ahead_diff(values, direction, beyond):
    length = values.shape[direction]
    ahead = jnp.concatenate([take_rows(values, direction, 1, length - 1), beyond], axis=direction)
    return ahead - values


def behind_diff(values, direction, before):
    length = values.shape[direction]
    behind = jnp.concatenate([before, take_rows(values, direction, 0, length - 1)], axis=direction)
    return values - behind


def rows_from_below(values, direction, stride, fill_value):
    length = values.shape[direction]
    padding = jnp.full_like(take_rows(values, direction, 0, stride), fill_value)
    return jnp.concatenate(
        [padding, take_rows(values, direction, 0, length - stride)], axis=direction
    )


def rows_from_above(values, direction, stride, fill_value):
    length = values.shape[direction]
    padding = jnp.full_like(take_rows(values, direction, 0, stride), fill_value)
    return jnp.concatenate(
        [take_rows(values, direction, stride, length - stride), padding], axis=direction
    )


def reduce_lines(lower_band, main_band, upper_band, right_side, direction):
    length = main_band.shape[direction]
    stride = 1
    while stride < length:
        low_lower = rows_from_below(lower_band, direction, stride, 0.0)
        low_main = rows_from_below(main_band, direction, stride, 1.0)
        low_upper = rows_from_below(upper_band, direction, stride, 0.0)
        low_right = rows_from_below(right_side, direction + 1, stride, 0.0)
        high_lower = rows_from_above(lower_band, direction, stride, 0.0)
        high_main = rows_from_above(main_band, direction, stride, 1.0)
        high_upper = rows_from_above(upper_band, direction, stride, 0.0)
        high_right = rows_from_above(right_side, direction + 1, stride, 0.0)
        ratio_low = -lower_band / low_main
        ratio_high = -upper_band / high_main
        right_side = right_side + ratio_low[None] * low_right + ratio_high[None] * high_right
        main_band = main_band + ratio_low * low_upper + ratio_high * high_lower
        lower_band = ratio_low * low_lower
        upper_band = ratio_high * high_upper
        stride = stride * 2
    return right_side / main_band[None]


def bands(coupling, damping, row_index, line_length):
    lower_band = jnp.where(row_index >= 1, -coupling, 0.0)
    upper_band = jnp.where(row_index <= line_length - 2, -coupling, 0.0)
    main_band = 1.0 + damping + coupling * jnp.where(row_index >= 1, 2.0, 1.0)
    return (lower_band, main_band, upper_band)


def cyclic_shift(values, axis, shift):
    count = lax.axis_size(axis)
    return lax.ppermute(values, axis, [(source, (source + shift) % count) for source in range(count)])


def gathered(values, axis):
    count = lax.axis_size(axis)
    if count in HOPS:
        direct, hop = HOPS[count]
        held = {0: values}
        for shift in direct:
            held[shift] = cyclic_shift(values, axis, shift)
        carried = [shift for shift in range(count) if shift + hop < count and shift + hop not in held]
        moved = cyclic_shift(jnp.stack([held[shift] for shift in carried]), axis, hop)
        for index, shift in enumerate(carried):
            held[shift + hop] = moved[index]
        return jnp.stack([held[shift] for shift in range(count)]), held
    direct = count if count <= LIMIT else DIRECT.get(count, (count + 1) // 2)
    pieces = [values] + [cyclic_shift(values, axis, shift) for shift in range(1, direct)]
    held = dict(enumerate(pieces))
    shifted = jnp.stack(pieces)
    while shifted.shape[0] < count:
        have = shifted.shape[0]
        moved = cyclic_shift(shifted[: count - have], axis, have)
        for index in range(moved.shape[0]):
            held[have + index] = moved[index]
        shifted = jnp.concatenate([shifted, moved])
    return shifted, held


def block_spikes(lower_band, main_band, upper_band, right_side, direction):
    length = main_band.shape[direction]
    row_index = lax.broadcasted_iota(jnp.int32, main_band.shape, direction)
    first_row = row_index == 0
    last_row = row_index == length - 1
    left_column = jnp.where(first_row, -lower_band, 0.0)
    right_column = jnp.where(last_row, -upper_band, 0.0)
    inner_lower = jnp.where(first_row, 0.0, lower_band)
    inner_upper = jnp.where(last_row, 0.0, upper_band)
    stacked = jnp.stack([right_side, left_column, right_column])
    return reduce_lines(inner_lower, main_band, inner_upper, stacked, direction)


def interface_sweep(coefficients, position):
    blocks = coefficients.shape[0]
    alpha = jnp.zeros_like(coefficients[0, 0])
    beta = jnp.zeros_like(alpha)
    handed = jnp.zeros_like(alpha)
    carried = []
    for block in range(blocks):
        held = lax.dynamic_index_in_dim(coefficients, (position - block) % blocks, 0, False)
        a0, a1, a2, b0, b1, b2, passed = [held[index] for index in range(7)]
        alpha = alpha + handed
        handed = passed
        scale = 1.0 / (1.0 - a1 * beta)
        p_term = (a0 + a1 * alpha) * scale
        q_term = a2 * scale
        carried.append((alpha, beta, p_term, q_term))
        alpha = b0 + b1 * (alpha + beta * p_term)
        beta = b1 * beta * q_term + b2
    following = jnp.zeros_like(alpha)
    firsts = [None] * blocks
    earlier_lasts = [None] * blocks
    for block in reversed(range(blocks)):
        alpha_before, beta_before, p_term, q_term = carried[block]
        first_value = p_term + q_term * following
        firsts[block] = first_value
        earlier_lasts[block] = alpha_before + beta_before * first_value
        following = first_value
    nexts = jnp.stack(firsts[1:] + [jnp.zeros_like(alpha)])
    earlier = jnp.stack(earlier_lasts)
    return (
        lax.dynamic_index_in_dim(earlier, position, 0, keepdims=False),
        lax.dynamic_index_in_dim(nexts, position, 0, keepdims=False),
    )


def partitioned(lower_band, main_band, upper_band, right_side, direction, axis, handed_on, extra):
    length = main_band.shape[direction]
    solved = block_spikes(lower_band, main_band, upper_band, right_side, direction)
    edges = jnp.concatenate(
        [
            take_rows(solved, direction + 1, 0, 1),
            take_rows(solved, direction + 1, length - 1, 1),
            handed_on,
            extra,
        ]
    )
    everyone, held = gathered(edges, axis)
    count = lax.axis_size(axis)
    position = lax.axis_index(axis)
    from_below = jnp.where(position >= 1, held[1][7], 0.0)
    from_above = jnp.where(position <= count - 2, held[count - 1][7], 0.0)
    return solved, everyone, from_below, from_above


def finished(solved, everyone, axis):
    earlier, following = interface_sweep(everyone, lax.axis_index(axis))
    return solved[0] + solved[1] * earlier + solved[2] * following, following


def body(
    electric_x,
    electric_y,
    electric_z,
    magnetic_x,
    magnetic_y,
    magnetic_z,
    permittivity,
    conductivity,
):
    coupling = step_ratio / permittivity
    damping = conductivity / permittivity
    keeping = 1.0 - damping
    size_y = electric_x.shape[0]
    size_z = electric_x.shape[1]
    size_x = electric_x.shape[2]
    cross_y = ahead_diff(electric_y, 2, edge_zeros(electric_y, 2))
    below_my = passed_along(take_rows(magnetic_y, 1, size_z - 1, 1), "gz", 1)
    above_ez = passed_along(take_rows(electric_z, 0, 0, 1), "gy", -1)
    cross_z = ahead_diff(electric_z, 0, above_ez)
    source_x = keeping * electric_x + coupling * (
        behind_diff(magnetic_z, 0, edge_zeros(magnetic_z, 0))
        - behind_diff(cross_y, 0, edge_zeros(cross_y, 0))
        - behind_diff(magnetic_y, 1, below_my)
    )
    source_y = keeping * electric_y + coupling * (
        behind_diff(magnetic_x, 1, edge_zeros(magnetic_x, 1))
        - behind_diff(cross_z, 1, edge_zeros(cross_z, 1))
        - behind_diff(magnetic_z, 2, edge_zeros(magnetic_z, 2))
    )
    index_z = lax.broadcasted_iota(jnp.int32, coupling.shape, 1) + lax.axis_index("gz") * size_z
    lower_z, main_z, upper_z = bands(coupling, damping, index_z, size_z * lax.axis_size("gz"))
    solved_z, everyone_z, _, above_ex = partitioned(
        lower_z,
        main_z,
        upper_z,
        source_y,
        1,
        "gz",
        (take_rows(cross_z, 1, size_z - 1, 1) - take_rows(magnetic_x, 1, size_z - 1, 1))[None],
        take_rows(electric_x, 1, 0, 1)[None],
    )
    index_y = lax.broadcasted_iota(jnp.int32, coupling.shape, 0) + lax.axis_index("gy") * size_y
    lower_y, main_y, upper_y = bands(coupling, damping, index_y, size_y * lax.axis_size("gy"))
    solved_y, everyone_y, below_mx, _ = partitioned(
        lower_y,
        main_y,
        upper_y,
        source_x,
        0,
        "gy",
        (take_rows(cross_y, 0, size_y - 1, 1) - take_rows(magnetic_z, 0, size_y - 1, 1))[None],
        take_rows(magnetic_x, 0, size_y - 1, 1)[None],
    )
    half_electric_x, fresh_ex = finished(solved_y, everyone_y, "gy")
    cross_x = ahead_diff(electric_x, 1, above_ex)
    source_z = keeping * electric_z + coupling * (
        behind_diff(magnetic_y, 2, edge_zeros(magnetic_y, 2))
        - behind_diff(cross_x, 2, edge_zeros(cross_x, 2))
        - behind_diff(magnetic_x, 0, below_mx)
    )
    index_x = lax.broadcasted_iota(jnp.int32, coupling.shape, 2)
    lower_x, main_x, upper_x = bands(coupling, damping, index_x, size_x)
    half_electric_z = reduce_lines(lower_x, main_x, upper_x, source_z[None], 2)[0]
    half_electric_z, everyone_z = lax.optimization_barrier((half_electric_z, everyone_z))
    half_electric_y, fresh_ey = finished(solved_z, everyone_z, "gz")
    half_magnetic_x = magnetic_x + ahead_diff(half_electric_y, 1, fresh_ey) - cross_z
    half_magnetic_y = (
        magnetic_y + ahead_diff(half_electric_z, 2, edge_zeros(half_electric_z, 2)) - cross_x
    )
    half_magnetic_z = magnetic_z + ahead_diff(half_electric_x, 0, fresh_ex) - cross_y
    return (
        half_electric_x,
        half_electric_y,
        half_electric_z,
        half_magnetic_x,
        half_magnetic_y,
        half_magnetic_z,
    )


def solution(mesh):
    placed = (P("gy", "gz", None),) * 8
    return jax.shard_map(
        body,
        mesh=mesh,
        in_specs=placed,
        out_specs=(P("gy", "gz", None),) * 6,
        check_vma=False,
    )
```
